256 devices in a mesh: ctx: 64 (over z, y_hi, x), head: 4 (over y_lo, core).
Axes of the slice: x: 4, y: 4 (y_hi: 2, y_lo: 2; y = y_hi * 2 + y_lo), z: 8, core: 2. Of those that a mesh axis runs over, the one named last changes fastest.
Arguments:
- query_rows: bfloat16 [32768, 5120], P(('ctx', 'head')), may hold values from -6 to 6
- key_rows: bfloat16 [32768, 1024], P(('ctx', 'head')), may hold values from -6 to 6
- value_rows: bfloat16 [32768, 1024], P(('ctx', 'head')), may hold values from -6 to 6
- attn_output: bfloat16 [32768, 5120], P(('ctx', 'head')), may hold values from -3 to 3
- out_grad: bfloat16 [32768, 5120], P(('ctx', 'head')), may hold values from -24 to 24
- log_norm: float32 [40, 32768], P('head', 'ctx'), may hold values from 5 to 7
- prefix_keys: bfloat16 [1024, 1024], P('ctx', 'head'), may hold values from -6 to 6
- prefix_values: bfloat16 [1024, 1024], P('ctx', 'head'), may hold values from -6 to 6
- response_blocks: int32 [128], replicated, may hold values from 1 to 16, as said below
- prompt_members: int32 [8, 16], replicated, may hold values from 0 to 127, as said below
Outputs:
- query_grad: bfloat16 [32768, 5120], P('ctx', 'head')
- key_grad: bfloat16 [32768, 1024], P('ctx', 'head')
- value_grad: bfloat16 [32768, 1024], P('ctx', 'head')
- prefix_keygrads: bfloat16 [1024, 1024], P('ctx', 'head')
- prefix_valuegrads: bfloat16 [1024, 1024], P('ctx', 'head')
The draws below stay inside these ranges and needn't reach their ends.
Inputs may be any that keep to these rules, and one draw needn't show every extreme that they name: `response_blocks`: the lengths fill all 1024 blocks of the row. Every index of ctx from 1 on begins inside a response that started on the index before it. `prompt_members`: every response, numbered 0 to 127 in order along the row, is listed exactly once.
All inputs are finite; a program needn't handle non-finite values.
Results may differ from the reference program's by a relative error of at most 0.008.
Values may be sent and summed in bfloat16 or wider, within the bound.
No kernel may reach another device: no remote copies, remote signals or barrier semaphores. Data moves between devices by JAX's collectives and lax.ppermute only.
A program may use at most 64 MiB of HBM per device.

```python
import math
import jax
import jax.numpy as jnp
from jax import lax

QH = 40
KVH = 8
HD = 128
TOK_DEV = 512
BLK = 32
PL = 128
GROUP = 16
TOKENS = 32768
NBD = 16
NB = 1024
NRESP = 128
NPROMPT = 8
N_CTX = 64


def draw_prompt_members(key, part):
    order = jax.random.permutation(key, NRESP)
    return order.reshape(NPROMPT, GROUP).astype(jnp.int32)


def draw_response_blocks(key, part):
    devices = NRESP // 2
    upper_key = jax.random.fold_in(key, 11)
    lower_key = jax.random.fold_in(key, 23)
    upper = jax.random.randint(upper_key, (devices,), 2, NBD).astype(jnp.int32)
    upper = upper.at[0].set(1)
    earlier = jnp.concatenate([jnp.ones((1,), jnp.int32), upper[:-1]])
    limit = jnp.maximum(jnp.minimum(earlier, upper - 1), 1).astype(jnp.int32)
    lower = jax.random.randint(lower_key, (devices,), 1, limit + 1).astype(jnp.int32)
    lower = lower.at[1].set(1)
    offsets = (jnp.arange(devices, dtype=jnp.int32) * NBD).astype(jnp.int32)
    inner = jnp.stack([offsets[1:] + lower[1:], offsets[1:] + upper[1:]], axis=1).reshape(-1)
    starts = jnp.concatenate([jnp.zeros((1,), jnp.int32), jnp.ones((1,), jnp.int32), inner.astype(jnp.int32)])
    ends = jnp.concatenate([starts[1:], jnp.full((1,), NB, jnp.int32)])
    return (ends - starts).astype(jnp.int32)


def block_scale(stream_key, shape, cuts, least, largest):
    factor_of, own = 1.0, jax.random.fold_in(stream_key, 6)
    for position, parts in cuts:
        steps = jnp.exp(jax.random.uniform(jax.random.fold_in(own, position), (parts,), jnp.float32, least / len(cuts), largest / len(cuts)))
        factor_of = factor_of * jnp.repeat(steps, shape[position] // parts).reshape([-1 if axis == position else 1 for axis in range(len(shape))])
    return factor_of


def normal_values(key, shape, spread, bound, split=(), kind=jnp.bfloat16):
    gain = block_scale(key, shape, split, -0.22, 0.18) if split else 1.0
    array = jax.random.normal(key, shape, jnp.float32) * spread * gain
    return jnp.minimum(jnp.maximum(array, -bound), bound).astype(kind)


def setup_inputs(seed: int = 0) -> dict:
    seeds = jax.random.split(jax.random.key(seed), 11)
    return {
        "query_rows": normal_values(seeds[0], (TOKENS, QH * HD), 1.0, 6.0, ((0, 256),)),
        "key_rows": normal_values(seeds[1], (TOKENS, KVH * HD), 1.0, 6.0, ((0, 256),)),
        "value_rows": normal_values(seeds[2], (TOKENS, KVH * HD), 1.0, 6.0, ((0, 256),)),
        "attn_output": normal_values(seeds[3], (TOKENS, QH * HD), 0.5, 3.0, ((0, 256),)),
        "out_grad": normal_values(seeds[4], (TOKENS, QH * HD), 4.0, 24.0, ((0, 256),)),
        "log_norm": jnp.clip(5.0 + 2.0 * jax.random.uniform(seeds[5], (QH, TOKENS), jnp.float32) ** block_scale(seeds[5], (QH, TOKENS), ((0, 4), (1, 64)), -0.2, 0.2), 5.0, 7.0),
        "prefix_keys": normal_values(seeds[6], (NPROMPT * PL, KVH * HD), 1.0, 6.0, ((0, 64), (1, 4))),
        "prefix_values": normal_values(seeds[7], (NPROMPT * PL, KVH * HD), 1.0, 6.0, ((0, 64), (1, 4))),
        "response_blocks": draw_response_blocks(jax.random.fold_in(seeds[10], 71), 0),
        "prompt_members": draw_prompt_members(jax.random.fold_in(seeds[10], 71), 0),
    }


def token_tables(response_blocks, prompt_members, first_block, count):
    lengths = response_blocks.astype(jnp.int32)
    starts = (jnp.cumsum(lengths) - lengths).astype(jnp.int32)
    responses = lengths.shape[0]
    group = prompt_members.shape[1]
    listed = prompt_members.reshape(-1).astype(jnp.int32)
    owner = (jnp.arange(listed.shape[0], dtype=jnp.int32) // group).astype(jnp.int32)
    numbers = jnp.arange(responses, dtype=jnp.int32)
    hits = listed[:, None] == numbers[None, :]
    prompt_of = lax.optimization_barrier(jnp.sum(jnp.where(hits, owner[:, None], 0), axis=0)).astype(jnp.int32)
    blocks = (first_block + jnp.arange(count, dtype=jnp.int32)).astype(jnp.int32)
    before = starts[None, :] <= blocks[:, None]
    first = lax.optimization_barrier(jnp.max(jnp.where(before, starts[None, :], 0), axis=1)).astype(jnp.int32)
    current = (lax.optimization_barrier(jnp.sum(before.astype(jnp.int32), axis=1)) - 1).astype(jnp.int32)
    chosen = numbers[None, :] == current[:, None]
    prompt_block = lax.optimization_barrier(jnp.sum(jnp.where(chosen, prompt_of[None, :], 0), axis=1)).astype(jnp.int32)
    return (jnp.repeat(first * BLK, BLK).astype(jnp.int32), jnp.repeat(prompt_block, BLK).astype(jnp.int32))

def tile_terms(queries, grads, norms, deltas, keys, values, allowed):
    rows = queries.shape[0]
    cols = keys.shape[0]
    heads = norms.shape[1]
    group = heads // (keys.shape[1] // HD)
    scale = 1.0 / math.sqrt(HD)

    def one_head(head, carry):
        query_acc, key_acc, value_acc = carry
        kv_head = head // group
        query_h = lax.dynamic_slice_in_dim(queries, head * HD, HD, 1)
        grad_h = lax.dynamic_slice_in_dim(grads, head * HD, HD, 1)
        key_h = lax.dynamic_slice_in_dim(keys, kv_head * HD, HD, 1)
        value_h = lax.dynamic_slice_in_dim(values, kv_head * HD, HD, 1)
        norm_h = lax.dynamic_slice_in_dim(norms, head, 1, 1)
        delta_h = lax.dynamic_slice_in_dim(deltas, head, 1, 1)
        logits = jnp.dot(query_h, key_h.T, preferred_element_type=jnp.float32)
        weights = jnp.where(allowed, jnp.exp(logits * scale - norm_h), 0.0)
        weights_b = weights.astype(jnp.bfloat16)
        value_term = jnp.dot(weights_b.T, grad_h, preferred_element_type=jnp.float32)
        dweights = jnp.dot(grad_h, value_h.T, preferred_element_type=jnp.float32)
        dlogits = (weights * (dweights - delta_h)).astype(jnp.bfloat16)
        query_term = jnp.dot(dlogits, key_h, preferred_element_type=jnp.float32)
        key_term = jnp.dot(dlogits.T, query_h, preferred_element_type=jnp.float32)
        query_acc = lax.dynamic_update_slice_in_dim(query_acc, query_term, head * HD, 1)
        old_key = lax.dynamic_slice_in_dim(key_acc, kv_head * HD, HD, 1)
        key_acc = lax.dynamic_update_slice_in_dim(key_acc, old_key + key_term, kv_head * HD, 1)
        old_value = lax.dynamic_slice_in_dim(value_acc, kv_head * HD, HD, 1)
        value_acc = lax.dynamic_update_slice_in_dim(value_acc, old_value + value_term, kv_head * HD, 1)
        return (query_acc, key_acc, value_acc)
    start = (jnp.zeros((rows, queries.shape[1]), jnp.float32), jnp.zeros((cols, keys.shape[1]), jnp.float32), jnp.zeros((cols, keys.shape[1]), jnp.float32))
    return lax.fori_loop(0, heads, one_head, start)

def add_rows(total, term, offset):
    old = lax.dynamic_slice_in_dim(total, offset, term.shape[0], 0)
    return lax.dynamic_update_slice_in_dim(total, old + term, offset, 0)

def reference(query_rows, key_rows, value_rows, attn_output, out_grad, log_norm, prefix_keys, prefix_values, response_blocks, prompt_members):
    kv_width = key_rows.shape[1]
    scale = 1.0 / math.sqrt(HD)
    positions = jnp.arange(TOK_DEV, dtype=jnp.int32)

    def block_step(carry, index):
        key_acc, value_acc, pkey_acc, pvalue_acc = carry
        base = (index * TOK_DEV).astype(jnp.int32)
        prior = (jnp.maximum(index - 1, 0) * TOK_DEV).astype(jnp.int32)
        queries = lax.dynamic_slice_in_dim(query_rows, base, TOK_DEV, 0)
        grads = lax.dynamic_slice_in_dim(out_grad, base, TOK_DEV, 0)
        outputs = lax.dynamic_slice_in_dim(attn_output, base, TOK_DEV, 0)
        norms = lax.dynamic_slice_in_dim(log_norm, base, TOK_DEV, 1).T
        deltas = jnp.einsum('thd,thd->th', grads.reshape(TOK_DEV, QH, HD).astype(jnp.float32), outputs.reshape(TOK_DEV, QH, HD).astype(jnp.float32))
        keys_here = lax.dynamic_slice_in_dim(key_rows, base, TOK_DEV, 0)
        values_here = lax.dynamic_slice_in_dim(value_rows, base, TOK_DEV, 0)
        keys_prior = lax.dynamic_slice_in_dim(key_rows, prior, TOK_DEV, 0)
        values_prior = lax.dynamic_slice_in_dim(value_rows, prior, TOK_DEV, 0)
        starts, prompts = token_tables(response_blocks, prompt_members, index * NBD, NBD)
        local_start = starts - base
        allowed_here = (positions[None, :] >= local_start[:, None]) & (positions[None, :] <= positions[:, None])
        allowed_prior = positions[None, :] - TOK_DEV >= local_start[:, None]
        query_one, key_one, value_one = tile_terms(queries, grads, norms, deltas, keys_here, values_here, allowed_here)
        query_two, key_two, value_two = tile_terms(queries, grads, norms, deltas, keys_prior, values_prior, allowed_prior)
        query_total = query_one + query_two

        def prompt_step(number, state):

            def compute(inner):
                total, pkeys, pvalues = inner
                keys_p = lax.dynamic_slice_in_dim(prefix_keys, number * PL, PL, 0)
                values_p = lax.dynamic_slice_in_dim(prefix_values, number * PL, PL, 0)
                allowed = jnp.broadcast_to((prompts == number)[:, None], (TOK_DEV, PL))
                query_p, key_p, value_p = tile_terms(queries, grads, norms, deltas, keys_p, values_p, allowed)
                return (total + query_p, add_rows(pkeys, key_p, number * PL), add_rows(pvalues, value_p, number * PL))
            return lax.cond(jnp.any(prompts == number), compute, lambda inner: inner, state)
        query_total, pkey_acc, pvalue_acc = lax.fori_loop(0, NPROMPT, prompt_step, (query_total, pkey_acc, pvalue_acc))
        key_acc = add_rows(add_rows(key_acc, key_one, base), key_two, prior)
        value_acc = add_rows(add_rows(value_acc, value_one, base), value_two, prior)
        return ((key_acc, value_acc, pkey_acc, pvalue_acc), (query_total * scale).astype(jnp.bfloat16))
    init = (jnp.zeros((TOKENS, kv_width), jnp.float32), jnp.zeros((TOKENS, kv_width), jnp.float32), jnp.zeros((NPROMPT * PL, kv_width), jnp.float32), jnp.zeros((NPROMPT * PL, kv_width), jnp.float32))
    carry, query_blocks = lax.scan(block_step, init, jnp.arange(N_CTX, dtype=jnp.int32))
    key_acc, value_acc, pkey_acc, pvalue_acc = carry
    query_grad = query_blocks.reshape(TOKENS, QH * HD)
    return (query_grad, (key_acc * scale).astype(jnp.bfloat16), value_acc.astype(jnp.bfloat16), (pkey_acc * scale).astype(jnp.bfloat16), pvalue_acc.astype(jnp.bfloat16))
```

```python
import math

import jax
import jax.numpy as jnp
import numpy as np
from jax import lax
from jax.sharding import Mesh
from jax.sharding import PartitionSpec as P

HD = 128
BLK = 32
PL = 128

CTX_PARTS = (("z", 8), ("yh", 2), ("x", 4))


def ctx_axes(mesh):
    ctx = mesh.shape["ctx"]
    if ctx == math.prod(n for _, n in CTX_PARTS):
        return CTX_PARTS
    return (("c", ctx),)


def shifted(array, axes, sizes, by):
    devices = math.prod(sizes)
    pairs = [(i, i + by) for i in range(devices) if 0 <= i + by < devices]
    return lax.ppermute(array, axes, pairs)


def block_tables(response_blocks, prompt_members, first_block, count):
    starts = jnp.cumsum(response_blocks) - response_blocks
    responses = response_blocks.shape[0]
    group = prompt_members.shape[1]
    listed = prompt_members.reshape(-1)
    owner = jnp.arange(listed.shape[0], dtype=jnp.int32) // group
    numbers = jnp.arange(responses, dtype=jnp.int32)
    hits = listed[:, None] == numbers[None, :]
    prompt_of = jnp.sum(jnp.where(hits, owner[:, None], 0), axis=0)
    blocks = first_block + jnp.arange(count, dtype=jnp.int32)
    before = starts[None, :] <= blocks[:, None]
    first = jnp.max(jnp.where(before, starts[None, :], 0), axis=1)
    current = jnp.sum(before.astype(jnp.int32), axis=1) - 1
    chosen = numbers[None, :] == current[:, None]
    prompt_block = jnp.sum(jnp.where(chosen, prompt_of[None, :], 0), axis=1)
    return first, prompt_block


def make_shards(parts):
    names = tuple(n for n, _ in parts)
    sizes = tuple(s for _, s in parts)

    def shards(
        query_rows,
        key_rows,
        value_rows,
        attn_output,
        out_grad,
        log_norm,
        prefix_keys,
        prefix_values,
        response_blocks,
        prompt_members,
    ):
        f32, bf16 = jnp.float32, jnp.bfloat16
        nh = lax.axis_size("head")
        rows, qw = query_rows.shape
        kw = key_rows.shape[1]
        all_heads = qw // HD
        scale = 1.0 / math.sqrt(HD)

        delta_rows = jnp.einsum(
            "thd,thd->th",
            out_grad.reshape(rows, all_heads, HD),
            attn_output.reshape(rows, all_heads, HD),
            preferred_element_type=f32,
        )
        packed = jnp.concatenate(
            [
                query_rows.reshape(rows, nh, qw // nh),
                out_grad.reshape(rows, nh, qw // nh),
                key_rows.reshape(rows, nh, kw // nh),
                value_rows.reshape(rows, nh, kw // nh),
            ],
            axis=2,
        )
        got = lax.all_to_all(packed, "head", split_axis=1, concat_axis=0, tiled=True)
        deltas = lax.all_to_all(
            delta_rows.reshape(rows, nh, all_heads // nh),
            "head",
            split_axis=1,
            concat_axis=0,
            tiled=True,
        )
        tokens = got.shape[0]
        got = got.reshape(tokens, -1)
        lq, lk = qw // nh, kw // nh
        kvh = lk // HD
        grp = (lq // HD) // kvh
        q = got[:, :lq].reshape(tokens, kvh, grp, HD)
        do = got[:, lq : 2 * lq].reshape(tokens, kvh, grp, HD)
        k = got[:, 2 * lq : 2 * lq + lk].reshape(tokens, kvh, HD)
        v = got[:, 2 * lq + lk :].reshape(tokens, kvh, HD)
        norms = log_norm.reshape(kvh, grp, tokens)
        delta = deltas.reshape(tokens, kvh * grp).T.reshape(kvh, grp, tokens)

        position = lax.axis_index(names)
        base = position * tokens
        nblk = tokens // BLK
        first, prompt_block = block_tables(
            response_blocks, prompt_members, position * nblk, nblk
        )
        local_start = jnp.repeat(first * BLK, BLK) - base

        k_prior, v_prior = shifted((k, v), names, sizes, 1)
        keys = jnp.concatenate([k_prior, k], axis=0)
        values = jnp.concatenate([v_prior, v], axis=0)
        u = jnp.arange(2 * tokens, dtype=jnp.int32) - tokens
        t = jnp.arange(tokens, dtype=jnp.int32)
        allowed = (u[None, :] >= local_start[:, None]) & (u[None, :] <= t[:, None])

        dq_parts, dk_parts, dv_parts = [], [], []
        for g in range(kvh):
            qg, dog, kg, vg = q[:, g], do[:, g], keys[:, g], values[:, g]
            logits = jnp.einsum("trd,sd->rts", qg, kg, preferred_element_type=f32)
            w = jnp.where(
                allowed[None], jnp.exp(logits * scale - norms[g][:, :, None]), 0.0
            )
            wb = w.astype(bf16)
            dv_parts.append(jnp.einsum("rts,trd->sd", wb, dog, preferred_element_type=f32))
            dw = jnp.einsum("trd,sd->rts", dog, vg, preferred_element_type=f32)
            dl = (w * (dw - delta[g][:, :, None])).astype(bf16)
            dq_parts.append(jnp.einsum("rts,sd->trd", dl, kg, preferred_element_type=f32))
            dk_parts.append(jnp.einsum("rts,trd->sd", dl, qg, preferred_element_type=f32))
        dq = jnp.stack(dq_parts, axis=1)
        dk = jnp.stack(dk_parts, axis=1)
        dv = jnp.stack(dv_parts, axis=1)

        pkv = jnp.concatenate([prefix_keys, prefix_values], axis=1)
        for name in reversed(names):
            pkv = lax.all_gather(pkv, name, axis=0, tiled=True)
        nprompt = pkv.shape[0] // PL
        pk_all = pkv[:, :lk].reshape(nprompt, PL, kvh, HD)
        pv_all = pkv[:, lk:].reshape(nprompt, PL, kvh, HD)
        pkb = jnp.take(pk_all, prompt_block, axis=0)
        pvb = jnp.take(pv_all, prompt_block, axis=0)
        qb = q.reshape(nblk, BLK, kvh, grp, HD)
        dob = do.reshape(nblk, BLK, kvh, grp, HD)
        normb = norms.reshape(kvh, grp, nblk, BLK).transpose(2, 0, 1, 3)
        deltab = delta.reshape(kvh, grp, nblk, BLK).transpose(2, 0, 1, 3)
        lp = jnp.einsum("bigrd,bjgd->bgrij", qb, pkb, preferred_element_type=f32)
        wp = jnp.exp(lp * scale - normb[..., None])
        wpb = wp.astype(bf16)
        dv_pb = jnp.einsum("bgrij,bigrd->bjgd", wpb, dob, preferred_element_type=f32)
        dwp = jnp.einsum("bigrd,bjgd->bgrij", dob, pvb, preferred_element_type=f32)
        dlp = (wp * (dwp - deltab[..., None])).astype(bf16)
        dq_p = jnp.einsum("bgrij,bjgd->bigrd", dlp, pkb, preferred_element_type=f32)
        dk_pb = jnp.einsum("bgrij,bigrd->bjgd", dlp, qb, preferred_element_type=f32)
        onehot = (prompt_block[:, None] == jnp.arange(nprompt)[None, :]).astype(f32)
        pgrad = jnp.einsum(
            "bp,bjx->pjx",
            onehot,
            jnp.concatenate(
                [dk_pb.reshape(nblk, PL, lk), dv_pb.reshape(nblk, PL, lk)], axis=2
            ),
            precision=lax.Precision.HIGHEST,
            preferred_element_type=f32,
        ).reshape(nprompt * PL, 2 * lk)
        for name in names:
            pgrad = lax.psum_scatter(pgrad, name, scatter_dimension=0, tiled=True)

        dq = dq + dq_p.reshape(tokens, kvh, grp, HD)
        back_k, back_v = shifted(
            (dk[:tokens].astype(bf16), dv[:tokens].astype(bf16)), names, sizes, -1
        )
        key_grad = (dk[tokens:] + back_k.astype(f32)) * scale
        value_grad = dv[tokens:] + back_v.astype(f32)
        return (
            (dq * scale).astype(bf16).reshape(tokens, lq),
            key_grad.astype(bf16).reshape(tokens, lk),
            value_grad.astype(bf16).reshape(tokens, lk),
            (pgrad[:, :lk] * scale).astype(bf16),
            pgrad[:, lk:].astype(bf16),
        )

    return shards, names


def solution(mesh):
    parts = ctx_axes(mesh)
    devices = np.asarray(mesh.devices).reshape(
        tuple(s for _, s in parts) + (mesh.shape["head"],)
    )
    sub = Mesh(devices, tuple(n for n, _ in parts) + ("head",))
    shards, ctx = make_shards(parts)
    rows = P(ctx + ("head",), None)
    grid = P(ctx, "head")
    placed = (
        rows,
        rows,
        rows,
        rows,
        rows,
        P("head", ctx),
        grid,
        grid,
        P(),
        P(),
    )
    return jax.shard_map(
        shards,
        mesh=sub,
        in_specs=placed,
        out_specs=(grid,) * 5,
        check_vma=False,
    )
```

```python
import math

import jax
import jax.numpy as jnp
import numpy as np
from jax import lax
from jax.sharding import Mesh
from jax.sharding import PartitionSpec as P

HD = 128
BLK = 32
PL = 128

CTX_PARTS = (("z", 8), ("yh", 2), ("x", 4))


def ctx_axes(mesh):
    ctx = mesh.shape["ctx"]
    if ctx == math.prod(n for _, n in CTX_PARTS):
        return CTX_PARTS
    return (("c", ctx),)


def shifted(array, axes, sizes, by):
    devices = math.prod(sizes)
    pairs = [(i, i + by) for i in range(devices) if 0 <= i + by < devices]
    return lax.ppermute(array, axes, pairs)


def block_tables(response_blocks, prompt_members, first_block, count):
    starts = jnp.cumsum(response_blocks) - response_blocks
    responses = response_blocks.shape[0]
    group = prompt_members.shape[1]
    listed = prompt_members.reshape(-1)
    owner = jnp.arange(listed.shape[0], dtype=jnp.int32) // group
    numbers = jnp.arange(responses, dtype=jnp.int32)
    hits = listed[:, None] == numbers[None, :]
    prompt_of = jnp.sum(jnp.where(hits, owner[:, None], 0), axis=0)
    blocks = first_block + jnp.arange(count, dtype=jnp.int32)
    before = starts[None, :] <= blocks[:, None]
    first = jnp.max(jnp.where(before, starts[None, :], 0), axis=1)
    current = jnp.sum(before.astype(jnp.int32), axis=1) - 1
    chosen = numbers[None, :] == current[:, None]
    prompt_block = jnp.sum(jnp.where(chosen, prompt_of[None, :], 0), axis=1)
    return first, prompt_block


def make_shards(parts):
    names = tuple(n for n, _ in parts)
    sizes = tuple(s for _, s in parts)

    def shards(
        query_rows,
        key_rows,
        value_rows,
        attn_output,
        out_grad,
        log_norm,
        prefix_keys,
        prefix_values,
        response_blocks,
        prompt_members,
    ):
        f32, bf16 = jnp.float32, jnp.bfloat16
        nh = lax.axis_size("head")
        rows, qw = query_rows.shape
        kw = key_rows.shape[1]
        all_heads = qw // HD
        scale = 1.0 / math.sqrt(HD)

        delta_rows = jnp.einsum(
            "thd,thd->th",
            out_grad.reshape(rows, all_heads, HD),
            attn_output.reshape(rows, all_heads, HD),
            preferred_element_type=f32,
        )
        packed = jnp.concatenate(
            [
                query_rows.reshape(rows, nh, qw // nh),
                out_grad.reshape(rows, nh, qw // nh),
                key_rows.reshape(rows, nh, kw // nh),
                value_rows.reshape(rows, nh, kw // nh),
            ],
            axis=2,
        )
        got = lax.all_to_all(packed, "head", split_axis=1, concat_axis=0, tiled=True)
        deltas = lax.all_to_all(
            delta_rows.reshape(rows, nh, all_heads // nh),
            "head",
            split_axis=1,
            concat_axis=0,
            tiled=True,
        )
        tokens = got.shape[0]
        got = got.reshape(tokens, -1)
        lq, lk = qw // nh, kw // nh
        kvh = lk // HD
        grp = (lq // HD) // kvh
        q = got[:, :lq].reshape(tokens, kvh, grp, HD)
        do = got[:, lq : 2 * lq].reshape(tokens, kvh, grp, HD)
        k = got[:, 2 * lq : 2 * lq + lk].reshape(tokens, kvh, HD)
        v = got[:, 2 * lq + lk :].reshape(tokens, kvh, HD)
        norms = log_norm.reshape(kvh, grp, tokens)
        delta = deltas.reshape(tokens, kvh * grp).T.reshape(kvh, grp, tokens)

        position = lax.axis_index(names)
        base = position * tokens
        nblk = tokens // BLK
        first, prompt_block = block_tables(
            response_blocks, prompt_members, position * nblk, nblk
        )
        local_start = jnp.repeat(first * BLK, BLK) - base

        k_prior, v_prior = shifted((k, v), names, sizes, 1)
        keys = jnp.concatenate([k_prior, k], axis=0)
        values = jnp.concatenate([v_prior, v], axis=0)
        u = jnp.arange(2 * tokens, dtype=jnp.int32) - tokens
        t = jnp.arange(tokens, dtype=jnp.int32)
        allowed = (u[None, :] >= local_start[:, None]) & (u[None, :] <= t[:, None])

        dq_parts, dk_parts, dv_parts = [], [], []
        for g in range(kvh):
            qg, dog, kg, vg = q[:, g], do[:, g], keys[:, g], values[:, g]
            logits = jnp.einsum("trd,sd->rts", qg, kg, preferred_element_type=f32)
            w = jnp.where(
                allowed[None], jnp.exp(logits * scale - norms[g][:, :, None]), 0.0
            )
            wb = w.astype(bf16)
            dv_parts.append(jnp.einsum("rts,trd->sd", wb, dog, preferred_element_type=f32))
            dw = jnp.einsum("trd,sd->rts", dog, vg, preferred_element_type=f32)
            dl = (w * (dw - delta[g][:, :, None])).astype(bf16)
            dq_parts.append(jnp.einsum("rts,sd->trd", dl, kg, preferred_element_type=f32))
            dk_parts.append(jnp.einsum("rts,trd->sd", dl, qg, preferred_element_type=f32))
        dq = jnp.stack(dq_parts, axis=1)
        dk = jnp.stack(dk_parts, axis=1)
        dv = jnp.stack(dv_parts, axis=1)

        pkv = jnp.concatenate([prefix_keys, prefix_values], axis=1)
        nctx = math.prod(sizes)
        pkv = lax.all_to_all(
            jnp.broadcast_to(pkv[None], (nctx,) + pkv.shape),
            names,
            split_axis=0,
            concat_axis=0,
            tiled=True,
        ).reshape(nctx * pkv.shape[0], pkv.shape[1])
        nprompt = pkv.shape[0] // PL
        pk_all = pkv[:, :lk].reshape(nprompt, PL, kvh, HD)
        pv_all = pkv[:, lk:].reshape(nprompt, PL, kvh, HD)
        pkb = jnp.take(pk_all, prompt_block, axis=0)
        pvb = jnp.take(pv_all, prompt_block, axis=0)
        qb = q.reshape(nblk, BLK, kvh, grp, HD)
        dob = do.reshape(nblk, BLK, kvh, grp, HD)
        normb = norms.reshape(kvh, grp, nblk, BLK).transpose(2, 0, 1, 3)
        deltab = delta.reshape(kvh, grp, nblk, BLK).transpose(2, 0, 1, 3)
        lp = jnp.einsum("bigrd,bjgd->bgrij", qb, pkb, preferred_element_type=f32)
        wp = jnp.exp(lp * scale - normb[..., None])
        wpb = wp.astype(bf16)
        dv_pb = jnp.einsum("bgrij,bigrd->bjgd", wpb, dob, preferred_element_type=f32)
        dwp = jnp.einsum("bigrd,bjgd->bgrij", dob, pvb, preferred_element_type=f32)
        dlp = (wp * (dwp - deltab[..., None])).astype(bf16)
        dq_p = jnp.einsum("bgrij,bjgd->bigrd", dlp, pkb, preferred_element_type=f32)
        dk_pb = jnp.einsum("bgrij,bigrd->bjgd", dlp, qb, preferred_element_type=f32)
        onehot = (prompt_block[:, None] == jnp.arange(nprompt)[None, :]).astype(f32)
        pgrad = jnp.einsum(
            "bp,bjx->pjx",
            onehot,
            jnp.concatenate(
                [dk_pb.reshape(nblk, PL, lk), dv_pb.reshape(nblk, PL, lk)], axis=2
            ),
            precision=lax.Precision.HIGHEST,
            preferred_element_type=f32,
        ).reshape(nprompt * PL, 2 * lk)
        pgrad = lax.all_to_all(
            pgrad.reshape(nctx, -1, pgrad.shape[1]),
            names,
            split_axis=0,
            concat_axis=0,
            tiled=True,
        ).sum(axis=0)

        dq = dq + dq_p.reshape(tokens, kvh, grp, HD)
        back_k, back_v = shifted(
            (dk[:tokens].astype(bf16), dv[:tokens].astype(bf16)), names, sizes, -1
        )
        key_grad = (dk[tokens:] + back_k.astype(f32)) * scale
        value_grad = dv[tokens:] + back_v.astype(f32)
        return (
            (dq * scale).astype(bf16).reshape(tokens, lq),
            key_grad.astype(bf16).reshape(tokens, lk),
            value_grad.astype(bf16).reshape(tokens, lk),
            (pgrad[:, :lk] * scale).astype(bf16),
            pgrad[:, lk:].astype(bf16),
        )

    return shards, names


def solution(mesh):
    parts = ctx_axes(mesh)
    devices = np.asarray(mesh.devices).reshape(
        tuple(s for _, s in parts) + (mesh.shape["head"],)
    )
    sub = Mesh(devices, tuple(n for n, _ in parts) + ("head",))
    shards, ctx = make_shards(parts)
    rows = P(ctx + ("head",), None)
    grid = P(ctx, "head")
    placed = (
        rows,
        rows,
        rows,
        rows,
        rows,
        P("head", ctx),
        grid,
        grid,
        P(),
        P(),
    )
    return jax.shard_map(
        shards,
        mesh=sub,
        in_specs=placed,
        out_specs=(grid,) * 5,
        check_vma=False,
    )
```

```python
import math

import jax
import jax.numpy as jnp
import numpy as np
from jax import lax
from jax.experimental import pallas as pl
from jax.experimental.pallas import tpu as pltpu
from jax.sharding import Mesh
from jax.sharding import PartitionSpec as P

HD = 128
BLK = 32
PL = 128

CTX_PARTS = (("z", 8), ("yh", 2), ("x", 4))


def ctx_axes(mesh):
    ctx = mesh.shape["ctx"]
    if ctx == math.prod(n for _, n in CTX_PARTS):
        return CTX_PARTS
    return (("c", ctx),)


def shifted(array, axes, sizes, by):
    devices = math.prod(sizes)
    pairs = [(i, i + by) for i in range(devices) if 0 <= i + by < devices]
    return lax.ppermute(array, axes, pairs)


def block_tables(response_blocks, prompt_members, first_block, count):
    starts = jnp.cumsum(response_blocks) - response_blocks
    responses = response_blocks.shape[0]
    group = prompt_members.shape[1]
    listed = prompt_members.reshape(-1)
    owner = jnp.arange(listed.shape[0], dtype=jnp.int32) // group
    numbers = jnp.arange(responses, dtype=jnp.int32)
    hits = listed[:, None] == numbers[None, :]
    prompt_of = jnp.sum(jnp.where(hits, owner[:, None], 0), axis=0)
    blocks = first_block + jnp.arange(count, dtype=jnp.int32)
    before = starts[None, :] <= blocks[:, None]
    first = jnp.max(jnp.where(before, starts[None, :], 0), axis=1)
    current = jnp.sum(before.astype(jnp.int32), axis=1) - 1
    chosen = numbers[None, :] == current[:, None]
    prompt_block = jnp.sum(jnp.where(chosen, prompt_of[None, :], 0), axis=1)
    return first, prompt_block


TT = 256


def tile_body(q_ref, do_ref, k_ref, v_ref, n_ref, d_ref, ls_ref, dq_ref, dk_ref, dv_ref):
    i = pl.program_id(1)
    f32, bf16 = jnp.float32, jnp.bfloat16
    scale = 1.0 / math.sqrt(HD)
    keys, values = k_ref[...], v_ref[...]
    span, rows = keys.shape[0], q_ref.shape[0]
    own = span // 2
    tok = i * rows + lax.broadcasted_iota(jnp.int32, (span, rows), 1)
    u = lax.broadcasted_iota(jnp.int32, (span, rows), 0) - own
    allowed = (u >= ls_ref[...]) & (u <= tok)
    nrm, dlt = n_ref[0], d_ref[0]
    nt = (((1,), (1,)), ((), ()))
    dk_acc = jnp.zeros((span, HD), f32)
    dv_acc = jnp.zeros((span, HD), f32)
    for r in range(nrm.shape[0]):
        cols = slice(r * HD, (r + 1) * HD)
        qr, dor = q_ref[:, cols], do_ref[:, cols]
        st = lax.dot_general(keys, qr, nt, preferred_element_type=f32)
        wt = jnp.where(allowed, jnp.exp(st * scale - nrm[r : r + 1, :]), 0.0)
        dv_acc = dv_acc + jnp.dot(wt.astype(bf16), dor, preferred_element_type=f32)
        dwt = lax.dot_general(values, dor, nt, preferred_element_type=f32)
        dlt_r = wt * (dwt - dlt[r : r + 1, :])
        dlb = dlt_r.astype(bf16)
        dk_acc = dk_acc + jnp.dot(dlb, qr, preferred_element_type=f32)
        dq_ref[:, cols] = jnp.dot(
            dlt_r.T.astype(bf16), keys, preferred_element_type=f32
        )

    @pl.when(i == 0)
    def _():
        dk_ref[...] = dk_acc
        dv_ref[...] = dv_acc

    @pl.when(i > 0)
    def _():
        dk_ref[...] += dk_acc
        dv_ref[...] += dv_acc


def tile_kernel(q, do, keys, values, norms, delta, local_start):
    tokens, lq = q.shape
    span, lk = keys.shape
    kvh, grp = norms.shape[0], norms.shape[1]
    rows = min(TT, tokens)
    width = grp * HD
    flops = 10 * tokens * span * HD * kvh * grp
    return pl.pallas_call(
        tile_body,
        grid=(kvh, tokens // rows),
        in_specs=[
            pl.BlockSpec((rows, width), lambda g, i: (i, g)),
            pl.BlockSpec((rows, width), lambda g, i: (i, g)),
            pl.BlockSpec((span, HD), lambda g, i: (0, g)),
            pl.BlockSpec((span, HD), lambda g, i: (0, g)),
            pl.BlockSpec((1, grp, rows), lambda g, i: (g, 0, i)),
            pl.BlockSpec((1, grp, rows), lambda g, i: (g, 0, i)),
            pl.BlockSpec((1, rows), lambda g, i: (0, i)),
        ],
        out_specs=[
            pl.BlockSpec((rows, width), lambda g, i: (i, g)),
            pl.BlockSpec((span, HD), lambda g, i: (0, g)),
            pl.BlockSpec((span, HD), lambda g, i: (0, g)),
        ],
        out_shape=[
            jax.ShapeDtypeStruct((tokens, lq), jnp.float32),
            jax.ShapeDtypeStruct((span, lk), jnp.float32),
            jax.ShapeDtypeStruct((span, lk), jnp.float32),
        ],
        compiler_params=pltpu.CompilerParams(
            dimension_semantics=("arbitrary", "arbitrary")
        ),
        cost_estimate=pl.CostEstimate(
            flops=flops,
            transcendentals=tokens * span * kvh * grp,
            bytes_accessed=4 * tokens * lq * 2 + 2 * span * lk * 5,
        ),
    )(q, do, keys, values, norms, delta, local_start)


def make_shards(parts):
    names = tuple(n for n, _ in parts)
    sizes = tuple(s for _, s in parts)

    def shards(
        query_rows,
        key_rows,
        value_rows,
        attn_output,
        out_grad,
        log_norm,
        prefix_keys,
        prefix_values,
        response_blocks,
        prompt_members,
    ):
        f32, bf16 = jnp.float32, jnp.bfloat16
        nh = lax.axis_size("head")
        rows, qw = query_rows.shape
        kw = key_rows.shape[1]
        all_heads = qw // HD
        scale = 1.0 / math.sqrt(HD)

        delta_rows = jnp.einsum(
            "thd,thd->th",
            out_grad.reshape(rows, all_heads, HD),
            attn_output.reshape(rows, all_heads, HD),
            preferred_element_type=f32,
        )
        packed = jnp.concatenate(
            [
                query_rows.reshape(rows, nh, qw // nh),
                out_grad.reshape(rows, nh, qw // nh),
                key_rows.reshape(rows, nh, kw // nh),
                value_rows.reshape(rows, nh, kw // nh),
            ],
            axis=2,
        )
        got = lax.all_to_all(packed, "head", split_axis=1, concat_axis=0, tiled=True)
        deltas = lax.all_to_all(
            delta_rows.reshape(rows, nh, all_heads // nh),
            "head",
            split_axis=1,
            concat_axis=0,
            tiled=True,
        )
        tokens = got.shape[0]
        got = got.reshape(tokens, -1)
        lq, lk = qw // nh, kw // nh
        kvh = lk // HD
        grp = (lq // HD) // kvh
        q = got[:, :lq].reshape(tokens, kvh, grp, HD)
        do = got[:, lq : 2 * lq].reshape(tokens, kvh, grp, HD)
        k = got[:, 2 * lq : 2 * lq + lk].reshape(tokens, kvh, HD)
        v = got[:, 2 * lq + lk :].reshape(tokens, kvh, HD)
        norms = log_norm.reshape(kvh, grp, tokens)
        delta = deltas.reshape(tokens, kvh * grp).T.reshape(kvh, grp, tokens)

        position = lax.axis_index(names)
        base = position * tokens
        nblk = tokens // BLK
        first, prompt_block = block_tables(
            response_blocks, prompt_members, position * nblk, nblk
        )
        local_start = jnp.repeat(first * BLK, BLK) - base

        k_prior, v_prior = shifted((k, v), names, sizes, 1)

        dq, dk, dv = tile_kernel(
            got[:, :lq],
            got[:, lq : 2 * lq],
            jnp.concatenate([k_prior, k], axis=0).reshape(2 * tokens, lk),
            jnp.concatenate([v_prior, v], axis=0).reshape(2 * tokens, lk),
            norms,
            delta,
            local_start.reshape(1, tokens).astype(jnp.int32),
        )
        dq = dq.reshape(tokens, kvh, grp, HD)
        dk = dk.reshape(2 * tokens, kvh, HD)
        dv = dv.reshape(2 * tokens, kvh, HD)

        pkv = jnp.concatenate([prefix_keys, prefix_values], axis=1)
        nctx = math.prod(sizes)
        pkv = lax.all_to_all(
            jnp.broadcast_to(pkv[None], (nctx,) + pkv.shape),
            names,
            split_axis=0,
            concat_axis=0,
            tiled=True,
        ).reshape(nctx * pkv.shape[0], pkv.shape[1])
        nprompt = pkv.shape[0] // PL
        pk_all = pkv[:, :lk].reshape(nprompt, PL, kvh, HD)
        pv_all = pkv[:, lk:].reshape(nprompt, PL, kvh, HD)
        pkb = jnp.take(pk_all, prompt_block, axis=0)
        pvb = jnp.take(pv_all, prompt_block, axis=0)
        qb = q.reshape(nblk, BLK, kvh, grp, HD)
        dob = do.reshape(nblk, BLK, kvh, grp, HD)
        normb = norms.reshape(kvh, grp, nblk, BLK).transpose(2, 0, 1, 3)
        deltab = delta.reshape(kvh, grp, nblk, BLK).transpose(2, 0, 1, 3)
        lp = jnp.einsum("bigrd,bjgd->bgrij", qb, pkb, preferred_element_type=f32)
        wp = jnp.exp(lp * scale - normb[..., None])
        wpb = wp.astype(bf16)
        dv_pb = jnp.einsum("bgrij,bigrd->bjgd", wpb, dob, preferred_element_type=f32)
        dwp = jnp.einsum("bigrd,bjgd->bgrij", dob, pvb, preferred_element_type=f32)
        dlp = (wp * (dwp - deltab[..., None])).astype(bf16)
        dq_p = jnp.einsum("bgrij,bjgd->bigrd", dlp, pkb, preferred_element_type=f32)
        dk_pb = jnp.einsum("bgrij,bigrd->bjgd", dlp, qb, preferred_element_type=f32)
        onehot = (prompt_block[:, None] == jnp.arange(nprompt)[None, :]).astype(f32)
        pgrad = jnp.einsum(
            "bp,bjx->pjx",
            onehot,
            jnp.concatenate(
                [dk_pb.reshape(nblk, PL, lk), dv_pb.reshape(nblk, PL, lk)], axis=2
            ),
            precision=lax.Precision.HIGHEST,
            preferred_element_type=f32,
        ).reshape(nprompt * PL, 2 * lk)
        pgrad = lax.all_to_all(
            pgrad.reshape(nctx, -1, pgrad.shape[1]),
            names,
            split_axis=0,
            concat_axis=0,
            tiled=True,
        ).sum(axis=0)

        dq = dq + dq_p.reshape(tokens, kvh, grp, HD)
        back_k, back_v = shifted(
            (dk[:tokens].astype(bf16), dv[:tokens].astype(bf16)), names, sizes, -1
        )
        key_grad = (dk[tokens:] + back_k.astype(f32)) * scale
        value_grad = dv[tokens:] + back_v.astype(f32)
        return (
            (dq * scale).astype(bf16).reshape(tokens, lq),
            key_grad.astype(bf16).reshape(tokens, lk),
            value_grad.astype(bf16).reshape(tokens, lk),
            (pgrad[:, :lk] * scale).astype(bf16),
            pgrad[:, lk:].astype(bf16),
        )

    return shards, names


def solution(mesh):
    parts = ctx_axes(mesh)
    devices = np.asarray(mesh.devices).reshape(
        tuple(s for _, s in parts) + (mesh.shape["head"],)
    )
    sub = Mesh(devices, tuple(n for n, _ in parts) + ("head",))
    shards, ctx = make_shards(parts)
    rows = P(ctx + ("head",), None)
    grid = P(ctx, "head")
    placed = (
        rows,
        rows,
        rows,
        rows,
        rows,
        P("head", ctx),
        grid,
        grid,
        P(),
        P(),
    )
    return jax.shard_map(
        shards,
        mesh=sub,
        in_specs=placed,
        out_specs=(grid,) * 5,
        check_vma=False,
    )
```

```python
import math

import jax
import jax.numpy as jnp
import numpy as np
from jax import lax
from jax.experimental import pallas as pl
from jax.experimental.pallas import tpu as pltpu
from jax.sharding import Mesh
from jax.sharding import PartitionSpec as P

HD = 128
BLK = 32
PL = 128

CTX_PARTS = (("z", 8), ("yh", 2), ("x", 4))


def ctx_axes(mesh):
    ctx = mesh.shape["ctx"]
    if ctx == math.prod(n for _, n in CTX_PARTS):
        return CTX_PARTS
    return (("c", ctx),)


def shifted(array, axes, sizes, by):
    devices = math.prod(sizes)
    pairs = [(i, i + by) for i in range(devices) if 0 <= i + by < devices]
    return lax.ppermute(array, axes, pairs)


def block_tables(response_blocks, prompt_members, first_block, count):
    starts = jnp.cumsum(response_blocks) - response_blocks
    responses = response_blocks.shape[0]
    group = prompt_members.shape[1]
    listed = prompt_members.reshape(-1)
    owner = jnp.arange(listed.shape[0], dtype=jnp.int32) // group
    numbers = jnp.arange(responses, dtype=jnp.int32)
    hits = listed[:, None] == numbers[None, :]
    prompt_of = jnp.sum(jnp.where(hits, owner[:, None], 0), axis=0)
    blocks = first_block + jnp.arange(count, dtype=jnp.int32)
    before = starts[None, :] <= blocks[:, None]
    first = jnp.max(jnp.where(before, starts[None, :], 0), axis=1)
    current = jnp.sum(before.astype(jnp.int32), axis=1) - 1
    chosen = numbers[None, :] == current[:, None]
    prompt_block = jnp.sum(jnp.where(chosen, prompt_of[None, :], 0), axis=1)
    return first, prompt_block


TT = 256


def tile_body(q_ref, do_ref, k_ref, v_ref, n_ref, d_ref, ls_ref, dq_ref, dk_ref, dv_ref):
    i = pl.program_id(1)
    f32, bf16 = jnp.float32, jnp.bfloat16
    scale = 1.0 / math.sqrt(HD)
    keys, values = k_ref[...], v_ref[...]
    span, rows = keys.shape[0], q_ref.shape[0]
    own = span // 2
    tok = i * rows + lax.broadcasted_iota(jnp.int32, (span, rows), 1)
    u = lax.broadcasted_iota(jnp.int32, (span, rows), 0) - own
    allowed = (u >= ls_ref[...]) & (u <= tok)
    nrm, dlt = n_ref[0], d_ref[0]
    nt = (((1,), (1,)), ((), ()))
    dk_acc = jnp.zeros((span, HD), f32)
    dv_acc = jnp.zeros((span, HD), f32)
    for r in range(nrm.shape[0]):
        cols = slice(r * HD, (r + 1) * HD)
        qr, dor = q_ref[:, cols], do_ref[:, cols]
        st = lax.dot_general(keys, qr, nt, preferred_element_type=f32)
        wt = jnp.where(allowed, jnp.exp(st * scale - nrm[r : r + 1, :]), 0.0)
        dv_acc = dv_acc + jnp.dot(wt.astype(bf16), dor, preferred_element_type=f32)
        dwt = lax.dot_general(values, dor, nt, preferred_element_type=f32)
        dlt_r = wt * (dwt - dlt[r : r + 1, :])
        dlb = dlt_r.astype(bf16)
        dk_acc = dk_acc + jnp.dot(dlb, qr, preferred_element_type=f32)
        dq_ref[:, cols] = jnp.dot(
            dlt_r.T.astype(bf16), keys, preferred_element_type=f32
        )

    @pl.when(i == 0)
    def _():
        dk_ref[...] = dk_acc
        dv_ref[...] = dv_acc

    @pl.when(i > 0)
    def _():
        dk_ref[...] += dk_acc
        dv_ref[...] += dv_acc


def tile_kernel(q, do, keys, values, norms, delta, local_start):
    tokens, lq = q.shape
    span, lk = keys.shape
    kvh, grp = norms.shape[0], norms.shape[1]
    rows = min(TT, tokens)
    width = grp * HD
    flops = 10 * tokens * span * HD * kvh * grp
    return pl.pallas_call(
        tile_body,
        grid=(kvh, tokens // rows),
        in_specs=[
            pl.BlockSpec((rows, width), lambda g, i: (i, g)),
            pl.BlockSpec((rows, width), lambda g, i: (i, g)),
            pl.BlockSpec((span, HD), lambda g, i: (0, g)),
            pl.BlockSpec((span, HD), lambda g, i: (0, g)),
            pl.BlockSpec((1, grp, rows), lambda g, i: (g, 0, i)),
            pl.BlockSpec((1, grp, rows), lambda g, i: (g, 0, i)),
            pl.BlockSpec((1, rows), lambda g, i: (0, i)),
        ],
        out_specs=[
            pl.BlockSpec((rows, width), lambda g, i: (i, g)),
            pl.BlockSpec((span, HD), lambda g, i: (0, g)),
            pl.BlockSpec((span, HD), lambda g, i: (0, g)),
        ],
        out_shape=[
            jax.ShapeDtypeStruct((tokens, lq), jnp.float32),
            jax.ShapeDtypeStruct((span, lk), jnp.float32),
            jax.ShapeDtypeStruct((span, lk), jnp.float32),
        ],
        compiler_params=pltpu.CompilerParams(
            dimension_semantics=("arbitrary", "arbitrary")
        ),
        cost_estimate=pl.CostEstimate(
            flops=flops,
            transcendentals=tokens * span * kvh * grp,
            bytes_accessed=4 * tokens * lq * 2 + 2 * span * lk * 5,
        ),
    )(q, do, keys, values, norms, delta, local_start)


def prompt_body(pb_ref, q_ref, do_ref, k_ref, v_ref, n_ref, d_ref, dk_ref, dv_ref, dq_ref):
    f32, bf16 = jnp.float32, jnp.bfloat16
    scale = 1.0 / math.sqrt(HD)
    nt = (((1,), (1,)), ((), ()))
    grp = n_ref.shape[2]
    dk_ref[...] = jnp.zeros_like(dk_ref)
    dv_ref[...] = jnp.zeros_like(dv_ref)

    def step(b, carry):
        rows = pl.ds(pl.multiple_of(b * BLK, BLK), BLK)
        keys_at = pl.ds(pl.multiple_of(pb_ref[b] * PL, PL), PL)
        kb, vb = k_ref[keys_at, :], v_ref[keys_at, :]
        nrm, dlt = n_ref[0, rows, :], d_ref[0, rows, :]
        dk_b = jnp.zeros((PL, HD), f32)
        dv_b = jnp.zeros((PL, HD), f32)
        for r in range(grp):
            cols = slice(r * HD, (r + 1) * HD)
            qr, dor = q_ref[rows, cols], do_ref[rows, cols]
            s = lax.dot_general(qr, kb, nt, preferred_element_type=f32)
            w = jnp.exp(s * scale - nrm[:, r : r + 1])
            dv_b = dv_b + jnp.dot(w.T.astype(bf16), dor, preferred_element_type=f32)
            dw = lax.dot_general(dor, vb, nt, preferred_element_type=f32)
            dl = w * (dw - dlt[:, r : r + 1])
            dq_ref[rows, cols] = jnp.dot(dl.astype(bf16), kb, preferred_element_type=f32)
            dk_b = dk_b + jnp.dot(dl.T.astype(bf16), qr, preferred_element_type=f32)
        dk_ref[keys_at, :] += dk_b
        dv_ref[keys_at, :] += dv_b
        return carry

    lax.fori_loop(0, pb_ref.shape[0], step, 0)


def prompt_kernel(q, do, pk, pv, norms, delta, prompt_block):
    tokens, lq = q.shape
    span, lk = pk.shape
    kvh, grp = norms.shape[0], norms.shape[2]
    width = grp * HD
    flops = 10 * tokens * PL * HD * kvh * grp
    grid_spec = pltpu.PrefetchScalarGridSpec(
        num_scalar_prefetch=1,
        grid=(kvh,),
        in_specs=[
            pl.BlockSpec((tokens, width), lambda g, pb: (0, g)),
            pl.BlockSpec((tokens, width), lambda g, pb: (0, g)),
            pl.BlockSpec((span, HD), lambda g, pb: (0, g)),
            pl.BlockSpec((span, HD), lambda g, pb: (0, g)),
            pl.BlockSpec((1, tokens, grp), lambda g, pb: (g, 0, 0)),
            pl.BlockSpec((1, tokens, grp), lambda g, pb: (g, 0, 0)),
        ],
        out_specs=[
            pl.BlockSpec((span, HD), lambda g, pb: (0, g)),
            pl.BlockSpec((span, HD), lambda g, pb: (0, g)),
            pl.BlockSpec((tokens, width), lambda g, pb: (0, g)),
        ],
    )
    return pl.pallas_call(
        prompt_body,
        grid_spec=grid_spec,
        out_shape=[
            jax.ShapeDtypeStruct((span, lk), jnp.float32),
            jax.ShapeDtypeStruct((span, lk), jnp.float32),
            jax.ShapeDtypeStruct((tokens, lq), jnp.float32),
        ],
        compiler_params=pltpu.CompilerParams(dimension_semantics=("arbitrary",)),
        cost_estimate=pl.CostEstimate(
            flops=flops,
            transcendentals=tokens * PL * kvh * grp,
            bytes_accessed=4 * tokens * lq * 2 + 4 * span * lk * 3,
        ),
    )(prompt_block, q, do, pk, pv, norms, delta)


def make_shards(parts):
    names = tuple(n for n, _ in parts)
    sizes = tuple(s for _, s in parts)

    def shards(
        query_rows,
        key_rows,
        value_rows,
        attn_output,
        out_grad,
        log_norm,
        prefix_keys,
        prefix_values,
        response_blocks,
        prompt_members,
    ):
        f32, bf16 = jnp.float32, jnp.bfloat16
        nh = lax.axis_size("head")
        rows, qw = query_rows.shape
        kw = key_rows.shape[1]
        all_heads = qw // HD
        scale = 1.0 / math.sqrt(HD)

        delta_rows = jnp.einsum(
            "thd,thd->th",
            out_grad.reshape(rows, all_heads, HD),
            attn_output.reshape(rows, all_heads, HD),
            preferred_element_type=f32,
        )
        packed = jnp.concatenate(
            [
                query_rows.reshape(rows, nh, qw // nh),
                out_grad.reshape(rows, nh, qw // nh),
                key_rows.reshape(rows, nh, kw // nh),
                value_rows.reshape(rows, nh, kw // nh),
            ],
            axis=2,
        )
        got = lax.all_to_all(packed, "head", split_axis=1, concat_axis=0, tiled=True)
        deltas = lax.all_to_all(
            delta_rows.reshape(rows, nh, all_heads // nh),
            "head",
            split_axis=1,
            concat_axis=0,
            tiled=True,
        )
        tokens = got.shape[0]
        got = got.reshape(tokens, -1)
        lq, lk = qw // nh, kw // nh
        kvh = lk // HD
        grp = (lq // HD) // kvh
        q = got[:, :lq].reshape(tokens, kvh, grp, HD)
        do = got[:, lq : 2 * lq].reshape(tokens, kvh, grp, HD)
        k = got[:, 2 * lq : 2 * lq + lk].reshape(tokens, kvh, HD)
        v = got[:, 2 * lq + lk :].reshape(tokens, kvh, HD)
        norms = log_norm.reshape(kvh, grp, tokens)
        delta = deltas.reshape(tokens, kvh * grp).T.reshape(kvh, grp, tokens)

        position = lax.axis_index(names)
        base = position * tokens
        nblk = tokens // BLK
        first, prompt_block = block_tables(
            response_blocks, prompt_members, position * nblk, nblk
        )
        local_start = jnp.repeat(first * BLK, BLK) - base

        k_prior, v_prior = shifted((k, v), names, sizes, 1)

        dq, dk, dv = tile_kernel(
            got[:, :lq],
            got[:, lq : 2 * lq],
            jnp.concatenate([k_prior, k], axis=0).reshape(2 * tokens, lk),
            jnp.concatenate([v_prior, v], axis=0).reshape(2 * tokens, lk),
            norms,
            delta,
            local_start.reshape(1, tokens).astype(jnp.int32),
        )
        dq = dq.reshape(tokens, kvh, grp, HD)
        dk = dk.reshape(2 * tokens, kvh, HD)
        dv = dv.reshape(2 * tokens, kvh, HD)

        pkv, _ = lax.optimization_barrier(
            (jnp.concatenate([prefix_keys, prefix_values], axis=1), got)
        )
        nctx = math.prod(sizes)
        pkv = lax.all_to_all(
            jnp.broadcast_to(pkv[None], (nctx,) + pkv.shape),
            names,
            split_axis=0,
            concat_axis=0,
            tiled=True,
        ).reshape(nctx * pkv.shape[0], pkv.shape[1])
        pgrad_k, pgrad_v, dq_p = prompt_kernel(
            got[:, :lq],
            got[:, lq : 2 * lq],
            pkv[:, :lk],
            pkv[:, lk:],
            norms.transpose(0, 2, 1),
            delta.transpose(0, 2, 1),
            prompt_block.astype(jnp.int32),
        )
        pgrad = jnp.concatenate([pgrad_k, pgrad_v], axis=1)
        pgrad = lax.all_to_all(
            pgrad.reshape(nctx, -1, pgrad.shape[1]),
            names,
            split_axis=0,
            concat_axis=0,
            tiled=True,
        ).sum(axis=0)

        dq = dq + dq_p.reshape(tokens, kvh, grp, HD)
        back_k, back_v = shifted(
            (dk[:tokens].astype(bf16), dv[:tokens].astype(bf16)), names, sizes, -1
        )
        key_grad = (dk[tokens:] + back_k.astype(f32)) * scale
        value_grad = dv[tokens:] + back_v.astype(f32)
        return (
            (dq * scale).astype(bf16).reshape(tokens, lq),
            key_grad.astype(bf16).reshape(tokens, lk),
            value_grad.astype(bf16).reshape(tokens, lk),
            (pgrad[:, :lk] * scale).astype(bf16),
            pgrad[:, lk:].astype(bf16),
        )

    return shards, names


def solution(mesh):
    parts = ctx_axes(mesh)
    devices = np.asarray(mesh.devices).reshape(
        tuple(s for _, s in parts) + (mesh.shape["head"],)
    )
    sub = Mesh(devices, tuple(n for n, _ in parts) + ("head",))
    shards, ctx = make_shards(parts)
    rows = P(ctx + ("head",), None)
    grid = P(ctx, "head")
    placed = (
        rows,
        rows,
        rows,
        rows,
        rows,
        P("head", ctx),
        grid,
        grid,
        P(),
        P(),
    )
    return jax.shard_map(
        shards,
        mesh=sub,
        in_specs=placed,
        out_specs=(grid,) * 5,
        check_vma=False,
    )
```

```python
import math

import jax
import jax.numpy as jnp
import numpy as np
from jax import lax
from jax.experimental import pallas as pl
from jax.experimental.pallas import tpu as pltpu
from jax.sharding import Mesh
from jax.sharding import PartitionSpec as P

HD = 128
BLK = 32
PL = 128

CTX_PARTS = (("z", 8), ("yh", 2), ("x", 4))


def ctx_axes(mesh):
    ctx = mesh.shape["ctx"]
    if ctx == math.prod(n for _, n in CTX_PARTS):
        return CTX_PARTS
    return (("c", ctx),)


def shifted(array, axes, sizes, by):
    devices = math.prod(sizes)
    pairs = [(i, i + by) for i in range(devices) if 0 <= i + by < devices]
    return lax.ppermute(array, axes, pairs)


def block_tables(response_blocks, prompt_members, first_block, count):
    starts = jnp.cumsum(response_blocks) - response_blocks
    responses = response_blocks.shape[0]
    group = prompt_members.shape[1]
    listed = prompt_members.reshape(-1)
    owner = jnp.arange(listed.shape[0], dtype=jnp.int32) // group
    numbers = jnp.arange(responses, dtype=jnp.int32)
    hits = listed[:, None] == numbers[None, :]
    prompt_of = jnp.sum(jnp.where(hits, owner[:, None], 0), axis=0)
    blocks = first_block + jnp.arange(count, dtype=jnp.int32)
    before = starts[None, :] <= blocks[:, None]
    first = jnp.max(jnp.where(before, starts[None, :], 0), axis=1)
    current = jnp.sum(before.astype(jnp.int32), axis=1) - 1
    chosen = numbers[None, :] == current[:, None]
    prompt_block = jnp.sum(jnp.where(chosen, prompt_of[None, :], 0), axis=1)
    return first, prompt_block


TT = 256


def tile_body(q_ref, do_ref, k_ref, v_ref, n_ref, d_ref, lo_ref, hi_ref, dq_ref, dk_ref, dv_ref):
    i = pl.program_id(1)
    f32, bf16 = jnp.float32, jnp.bfloat16
    scale = 1.0 / math.sqrt(HD)
    keys, values = k_ref[...], v_ref[...]
    span, rows = keys.shape[0], q_ref.shape[0]
    u = lax.broadcasted_iota(jnp.int32, (span, rows), 0)
    allowed = (u >= lo_ref[...]) & (u <= hi_ref[...])
    nrm, dlt = n_ref[0], d_ref[0]
    nt = (((1,), (1,)), ((), ()))
    dk_acc = jnp.zeros((span, HD), f32)
    dv_acc = jnp.zeros((span, HD), f32)
    for r in range(nrm.shape[0]):
        cols = slice(r * HD, (r + 1) * HD)
        qr, dor = q_ref[:, cols], do_ref[:, cols]
        st = lax.dot_general(keys, qr, nt, preferred_element_type=f32)
        wt = jnp.where(allowed, jnp.exp(st * scale - nrm[r : r + 1, :]), 0.0)
        dv_acc = dv_acc + jnp.dot(wt.astype(bf16), dor, preferred_element_type=f32)
        dwt = lax.dot_general(values, dor, nt, preferred_element_type=f32)
        dlt_r = wt * (dwt - dlt[r : r + 1, :])
        dlb = dlt_r.astype(bf16)
        dk_acc = dk_acc + jnp.dot(dlb, qr, preferred_element_type=f32)
        dq_ref[:, cols] = jnp.dot(
            dlt_r.T.astype(bf16), keys, preferred_element_type=f32
        )

    @pl.when(i == 0)
    def _():
        dk_ref[...] = dk_acc
        dv_ref[...] = dv_acc

    @pl.when(i > 0)
    def _():
        dk_ref[...] += dk_acc
        dv_ref[...] += dv_acc


def tile_kernel(q, do, keys, values, norms, delta, lo, hi):
    tokens, lq = q.shape
    span, lk = keys.shape
    kvh, grp = norms.shape[0], norms.shape[1]
    rows = min(TT, tokens)
    width = grp * HD
    flops = 10 * tokens * span * HD * kvh * grp
    return pl.pallas_call(
        tile_body,
        grid=(kvh, tokens // rows),
        in_specs=[
            pl.BlockSpec((rows, width), lambda g, i: (i, g)),
            pl.BlockSpec((rows, width), lambda g, i: (i, g)),
            pl.BlockSpec((span, HD), lambda g, i: (0, g)),
            pl.BlockSpec((span, HD), lambda g, i: (0, g)),
            pl.BlockSpec((1, grp, rows), lambda g, i: (g, 0, i)),
            pl.BlockSpec((1, grp, rows), lambda g, i: (g, 0, i)),
            pl.BlockSpec((1, rows), lambda g, i: (0, i)),
            pl.BlockSpec((1, rows), lambda g, i: (0, i)),
        ],
        out_specs=[
            pl.BlockSpec((rows, width), lambda g, i: (i, g)),
            pl.BlockSpec((span, HD), lambda g, i: (0, g)),
            pl.BlockSpec((span, HD), lambda g, i: (0, g)),
        ],
        out_shape=[
            jax.ShapeDtypeStruct((tokens, lq), jnp.float32),
            jax.ShapeDtypeStruct((span, lk), jnp.float32),
            jax.ShapeDtypeStruct((span, lk), jnp.float32),
        ],
        compiler_params=pltpu.CompilerParams(
            dimension_semantics=("arbitrary", "arbitrary")
        ),
        cost_estimate=pl.CostEstimate(
            flops=flops,
            transcendentals=tokens * span * kvh * grp,
            bytes_accessed=4 * tokens * lq * 2 + 2 * span * lk * 5,
        ),
    )(q, do, keys, values, norms, delta, lo, hi)


def make_shards(parts):
    names = tuple(n for n, _ in parts)
    sizes = tuple(s for _, s in parts)

    def shards(
        query_rows,
        key_rows,
        value_rows,
        attn_output,
        out_grad,
        log_norm,
        prefix_keys,
        prefix_values,
        response_blocks,
        prompt_members,
    ):
        f32, bf16 = jnp.float32, jnp.bfloat16
        nh = lax.axis_size("head")
        rows, qw = query_rows.shape
        kw = key_rows.shape[1]
        all_heads = qw // HD
        scale = 1.0 / math.sqrt(HD)

        delta_rows = jnp.einsum(
            "thd,thd->th",
            out_grad.reshape(rows, all_heads, HD),
            attn_output.reshape(rows, all_heads, HD),
            preferred_element_type=f32,
        )
        packed = jnp.concatenate(
            [
                query_rows.reshape(rows, nh, qw // nh),
                out_grad.reshape(rows, nh, qw // nh),
                key_rows.reshape(rows, nh, kw // nh),
                value_rows.reshape(rows, nh, kw // nh),
            ],
            axis=2,
        )
        got = lax.all_to_all(packed, "head", split_axis=1, concat_axis=0, tiled=True)
        deltas = lax.all_to_all(
            delta_rows.reshape(rows, nh, all_heads // nh),
            "head",
            split_axis=1,
            concat_axis=0,
            tiled=True,
        )
        tokens = got.shape[0]
        got = got.reshape(tokens, -1)
        lq, lk = qw // nh, kw // nh
        kvh = lk // HD
        grp = (lq // HD) // kvh
        q = got[:, :lq].reshape(tokens, kvh, grp, HD)
        do = got[:, lq : 2 * lq].reshape(tokens, kvh, grp, HD)
        k = got[:, 2 * lq : 2 * lq + lk].reshape(tokens, kvh, HD)
        v = got[:, 2 * lq + lk :].reshape(tokens, kvh, HD)
        norms = log_norm.reshape(kvh, grp, tokens)
        delta = deltas.reshape(tokens, kvh * grp).T.reshape(kvh, grp, tokens)

        position = lax.axis_index(names)
        base = position * tokens
        nblk = tokens // BLK
        first, prompt_block = block_tables(
            response_blocks, prompt_members, position * nblk, nblk
        )
        local_start = jnp.repeat(first * BLK, BLK) - base

        k_prior, v_prior = shifted((k, v), names, sizes, 1)

        dq, dk, dv = tile_kernel(
            got[:, :lq],
            got[:, lq : 2 * lq],
            jnp.concatenate([k_prior, k], axis=0).reshape(2 * tokens, lk),
            jnp.concatenate([v_prior, v], axis=0).reshape(2 * tokens, lk),
            norms,
            delta,
            (local_start + tokens).reshape(1, tokens).astype(jnp.int32),
            (jnp.arange(tokens, dtype=jnp.int32) + tokens).reshape(1, tokens),
        )
        dq = dq.reshape(tokens, kvh, grp, HD)
        dk = dk.reshape(2 * tokens, kvh, HD)
        dv = dv.reshape(2 * tokens, kvh, HD)

        pkv, _ = lax.optimization_barrier(
            (jnp.concatenate([prefix_keys, prefix_values], axis=1), got)
        )
        nctx = math.prod(sizes)
        pkv = lax.all_to_all(
            jnp.broadcast_to(pkv[None], (nctx,) + pkv.shape),
            names,
            split_axis=0,
            concat_axis=0,
            tiled=True,
        ).reshape(nctx * pkv.shape[0], pkv.shape[1])
        pkv, dq = lax.optimization_barrier((pkv, dq))
        prompt_lo = (jnp.repeat(prompt_block, BLK) * PL).astype(jnp.int32)
        dq_p, pgrad_k, pgrad_v = tile_kernel(
            got[:, :lq],
            got[:, lq : 2 * lq],
            pkv[:, :lk],
            pkv[:, lk:],
            norms,
            delta,
            prompt_lo.reshape(1, tokens),
            (prompt_lo + PL - 1).reshape(1, tokens),
        )
        pgrad = jnp.concatenate([pgrad_k, pgrad_v], axis=1)
        pgrad = lax.all_to_all(
            pgrad.reshape(nctx, -1, pgrad.shape[1]),
            names,
            split_axis=0,
            concat_axis=0,
            tiled=True,
        ).sum(axis=0)

        dq = dq + dq_p.reshape(tokens, kvh, grp, HD)
        back_k, back_v = shifted(
            (dk[:tokens].astype(bf16), dv[:tokens].astype(bf16)), names, sizes, -1
        )
        key_grad = (dk[tokens:] + back_k.astype(f32)) * scale
        value_grad = dv[tokens:] + back_v.astype(f32)
        return (
            (dq * scale).astype(bf16).reshape(tokens, lq),
            key_grad.astype(bf16).reshape(tokens, lk),
            value_grad.astype(bf16).reshape(tokens, lk),
            (pgrad[:, :lk] * scale).astype(bf16),
            pgrad[:, lk:].astype(bf16),
        )

    return shards, names


def solution(mesh):
    parts = ctx_axes(mesh)
    devices = np.asarray(mesh.devices).reshape(
        tuple(s for _, s in parts) + (mesh.shape["head"],)
    )
    sub = Mesh(devices, tuple(n for n, _ in parts) + ("head",))
    shards, ctx = make_shards(parts)
    rows = P(ctx + ("head",), None)
    grid = P(ctx, "head")
    placed = (
        rows,
        rows,
        rows,
        rows,
        rows,
        P("head", ctx),
        grid,
        grid,
        P(),
        P(),
    )
    return jax.shard_map(
        shards,
        mesh=sub,
        in_specs=placed,
        out_specs=(grid,) * 5,
        check_vma=False,
    )
```

```python
import math

import jax
import jax.numpy as jnp
import numpy as np
from jax import lax
from jax.experimental import pallas as pl
from jax.experimental.pallas import tpu as pltpu
from jax.sharding import Mesh
from jax.sharding import PartitionSpec as P

HD = 128
BLK = 32
PL = 128

CTX_PARTS = (("z", 8), ("yh", 2), ("x", 4))


def ctx_axes(mesh):
    ctx = mesh.shape["ctx"]
    if ctx == math.prod(n for _, n in CTX_PARTS):
        return CTX_PARTS
    return (("c", ctx),)


def shifted(array, axes, sizes, by):
    devices = math.prod(sizes)
    pairs = [(i, i + by) for i in range(devices) if 0 <= i + by < devices]
    return lax.ppermute(array, axes, pairs)


def block_tables(response_blocks, prompt_members, first_block, count):
    starts = jnp.cumsum(response_blocks) - response_blocks
    responses = response_blocks.shape[0]
    group = prompt_members.shape[1]
    listed = prompt_members.reshape(-1)
    owner = jnp.arange(listed.shape[0], dtype=jnp.int32) // group
    numbers = jnp.arange(responses, dtype=jnp.int32)
    hits = listed[:, None] == numbers[None, :]
    prompt_of = jnp.sum(jnp.where(hits, owner[:, None], 0), axis=0)
    blocks = first_block + jnp.arange(count, dtype=jnp.int32)
    before = starts[None, :] <= blocks[:, None]
    first = jnp.max(jnp.where(before, starts[None, :], 0), axis=1)
    current = jnp.sum(before.astype(jnp.int32), axis=1) - 1
    chosen = numbers[None, :] == current[:, None]
    prompt_block = jnp.sum(jnp.where(chosen, prompt_of[None, :], 0), axis=1)
    return first, prompt_block


CH = 128


def tile_body(need_ref, q_ref, do_ref, k_ref, v_ref, n_ref, d_ref, lo_ref, hi_ref, dq_ref, dkv_ref):
    f32, bf16 = jnp.float32, jnp.bfloat16
    scale = 1.0 / math.sqrt(HD)
    nt = (((1,), (1,)), ((), ()))
    rows, span, grp = q_ref.shape[0], k_ref.shape[0], n_ref.shape[1]
    nrm, dlt = n_ref[0], d_ref[0]
    lo, hi = lo_ref[...], hi_ref[...]
    dq_ref[...] = jnp.zeros_like(dq_ref)
    for c in range(span // CH):
        ks = slice(c * CH, (c + 1) * CH)

        @pl.when(need_ref[c] > 0)
        def _():
            keys, values = k_ref[ks, :], v_ref[ks, :]
            u = c * CH + lax.broadcasted_iota(jnp.int32, (CH, rows), 0)
            allowed = (u >= lo) & (u <= hi)
            dk_acc = jnp.zeros((CH, HD), f32)
            dv_acc = jnp.zeros((CH, HD), f32)
            for r in range(grp):
                cols = slice(r * HD, (r + 1) * HD)
                qr, dor = q_ref[:, cols], do_ref[:, cols]
                st = lax.dot_general(keys, qr, nt, preferred_element_type=f32)
                wt = jnp.where(allowed, jnp.exp(st * scale - nrm[r : r + 1, :]), 0.0)
                dv_acc = dv_acc + jnp.dot(wt.astype(bf16), dor, preferred_element_type=f32)
                dwt = lax.dot_general(values, dor, nt, preferred_element_type=f32)
                dlt_r = wt * (dwt - dlt[r : r + 1, :])
                dk_acc = dk_acc + jnp.dot(dlt_r.astype(bf16), qr, preferred_element_type=f32)
                dq_ref[:, cols] += jnp.dot(
                    dlt_r.T.astype(bf16), keys, preferred_element_type=f32
                )
            dkv_ref[ks, 0:HD] = dk_acc
            dkv_ref[ks, HD : 2 * HD] = dv_acc

        @pl.when(need_ref[c] == 0)
        def _():
            dkv_ref[ks, :] = jnp.zeros((CH, 2 * HD), f32)


def tile_kernel(q, do, keys, values, norms, delta, lo, hi):
    tokens, lq = q.shape
    span, lk = keys.shape
    kvh, grp = norms.shape[0], norms.shape[1]
    width = grp * HD
    starts = jnp.arange(span // CH, dtype=jnp.int32) * CH
    need = jnp.any(
        (lo.reshape(-1)[None, :] <= starts[:, None] + CH - 1)
        & (hi.reshape(-1)[None, :] >= starts[:, None]),
        axis=1,
    ).astype(jnp.int32)
    flops = 10 * tokens * span * HD * kvh * grp
    grid_spec = pltpu.PrefetchScalarGridSpec(
        num_scalar_prefetch=1,
        grid=(kvh,),
        in_specs=[
            pl.BlockSpec((tokens, width), lambda g, n: (0, g)),
            pl.BlockSpec((tokens, width), lambda g, n: (0, g)),
            pl.BlockSpec((span, HD), lambda g, n: (0, g)),
            pl.BlockSpec((span, HD), lambda g, n: (0, g)),
            pl.BlockSpec((1, grp, tokens), lambda g, n: (g, 0, 0)),
            pl.BlockSpec((1, grp, tokens), lambda g, n: (g, 0, 0)),
            pl.BlockSpec((1, tokens), lambda g, n: (0, 0)),
            pl.BlockSpec((1, tokens), lambda g, n: (0, 0)),
        ],
        out_specs=[
            pl.BlockSpec((tokens, width), lambda g, n: (0, g)),
            pl.BlockSpec((span, 2 * HD), lambda g, n: (0, g)),
        ],
    )
    return pl.pallas_call(
        tile_body,
        grid_spec=grid_spec,
        out_shape=[
            jax.ShapeDtypeStruct((tokens, lq), jnp.float32),
            jax.ShapeDtypeStruct((span, 2 * lk), jnp.float32),
        ],
        compiler_params=pltpu.CompilerParams(dimension_semantics=("arbitrary",)),
        cost_estimate=pl.CostEstimate(
            flops=flops,
            transcendentals=tokens * span * kvh * grp,
            bytes_accessed=4 * tokens * lq * 2 + 2 * span * lk * 6,
        ),
    )(need, q, do, keys, values, norms, delta, lo, hi)


def make_shards(parts):
    names = tuple(n for n, _ in parts)
    sizes = tuple(s for _, s in parts)

    def shards(
        query_rows,
        key_rows,
        value_rows,
        attn_output,
        out_grad,
        log_norm,
        prefix_keys,
        prefix_values,
        response_blocks,
        prompt_members,
    ):
        f32, bf16 = jnp.float32, jnp.bfloat16
        nh = lax.axis_size("head")
        rows, qw = query_rows.shape
        kw = key_rows.shape[1]
        all_heads = qw // HD
        scale = 1.0 / math.sqrt(HD)

        delta_rows = jnp.einsum(
            "thd,thd->th",
            out_grad.reshape(rows, all_heads, HD),
            attn_output.reshape(rows, all_heads, HD),
            preferred_element_type=f32,
        )
        packed = jnp.concatenate(
            [
                query_rows.reshape(rows, nh, qw // nh),
                out_grad.reshape(rows, nh, qw // nh),
                key_rows.reshape(rows, nh, kw // nh),
                value_rows.reshape(rows, nh, kw // nh),
            ],
            axis=2,
        )
        got = lax.all_to_all(packed, "head", split_axis=1, concat_axis=0, tiled=True)
        deltas = lax.all_to_all(
            delta_rows.reshape(rows, nh, all_heads // nh),
            "head",
            split_axis=1,
            concat_axis=0,
            tiled=True,
        )
        tokens = got.shape[0]
        got = got.reshape(tokens, -1)
        lq, lk = qw // nh, kw // nh
        kvh = lk // HD
        grp = (lq // HD) // kvh
        q = got[:, :lq].reshape(tokens, kvh, grp, HD)
        do = got[:, lq : 2 * lq].reshape(tokens, kvh, grp, HD)
        k = got[:, 2 * lq : 2 * lq + lk].reshape(tokens, kvh, HD)
        v = got[:, 2 * lq + lk :].reshape(tokens, kvh, HD)
        norms = log_norm.reshape(kvh, grp, tokens)
        delta = deltas.reshape(tokens, kvh * grp).T.reshape(kvh, grp, tokens)

        position = lax.axis_index(names)
        base = position * tokens
        nblk = tokens // BLK
        first, prompt_block = block_tables(
            response_blocks, prompt_members, position * nblk, nblk
        )
        local_start = jnp.repeat(first * BLK, BLK) - base

        kv = got[:, 2 * lq :]
        kv_prior = shifted(kv, names, sizes, 1)
        dq, dkv = tile_kernel(
            got[:, :lq],
            got[:, lq : 2 * lq],
            jnp.concatenate([kv_prior[:, :lk], kv[:, :lk]], axis=0),
            jnp.concatenate([kv_prior[:, lk:], kv[:, lk:]], axis=0),
            norms,
            delta,
            (local_start + tokens).reshape(1, tokens).astype(jnp.int32),
            (jnp.arange(tokens, dtype=jnp.int32) + tokens).reshape(1, tokens),
        )

        pkv, _ = lax.optimization_barrier(
            (jnp.concatenate([prefix_keys, prefix_values], axis=1), got)
        )
        nctx = math.prod(sizes)
        pkv = lax.all_to_all(
            jnp.broadcast_to(pkv[None], (nctx,) + pkv.shape),
            names,
            split_axis=0,
            concat_axis=0,
            tiled=True,
        ).reshape(nctx * pkv.shape[0], pkv.shape[1])
        pkv, dq = lax.optimization_barrier((pkv, dq))
        prompt_lo = (jnp.repeat(prompt_block, BLK) * PL).astype(jnp.int32)
        dq_p, pgrad = tile_kernel(
            got[:, :lq],
            got[:, lq : 2 * lq],
            pkv[:, :lk],
            pkv[:, lk:],
            norms,
            delta,
            prompt_lo.reshape(1, tokens),
            (prompt_lo + PL - 1).reshape(1, tokens),
        )
        pgrad = lax.all_to_all(
            pgrad.reshape(nctx, -1, pgrad.shape[1]),
            names,
            split_axis=0,
            concat_axis=0,
            tiled=True,
        ).sum(axis=0)
        pgrad = pgrad.reshape(-1, kvh, 2, HD)

        back = shifted(dkv[:tokens].astype(bf16), names, sizes, -1)
        kv_grad = (dkv[tokens:] + back.astype(f32)).reshape(tokens, kvh, 2, HD)
        return (
            ((dq + dq_p) * scale).astype(bf16),
            (kv_grad[:, :, 0] * scale).astype(bf16).reshape(tokens, lk),
            kv_grad[:, :, 1].astype(bf16).reshape(tokens, lk),
            (pgrad[:, :, 0] * scale).astype(bf16).reshape(-1, lk),
            pgrad[:, :, 1].astype(bf16).reshape(-1, lk),
        )

    return shards, names


def solution(mesh):
    parts = ctx_axes(mesh)
    devices = np.asarray(mesh.devices).reshape(
        tuple(s for _, s in parts) + (mesh.shape["head"],)
    )
    sub = Mesh(devices, tuple(n for n, _ in parts) + ("head",))
    shards, ctx = make_shards(parts)
    rows = P(ctx + ("head",), None)
    grid = P(ctx, "head")
    placed = (
        rows,
        rows,
        rows,
        rows,
        rows,
        P("head", ctx),
        grid,
        grid,
        P(),
        P(),
    )
    return jax.shard_map(
        shards,
        mesh=sub,
        in_specs=placed,
        out_specs=(grid,) * 5,
        check_vma=False,
    )
```

```python
import math

import jax
import jax.numpy as jnp
import numpy as np
from jax import lax
from jax.experimental import pallas as pl
from jax.experimental.pallas import tpu as pltpu
from jax.sharding import Mesh
from jax.sharding import PartitionSpec as P

HD = 128
BLK = 32
PL = 128

CTX_PARTS = (("z", 8), ("yh", 2), ("x", 4))


def ctx_axes(mesh):
    ctx = mesh.shape["ctx"]
    if ctx == math.prod(n for _, n in CTX_PARTS):
        return CTX_PARTS
    return (("c", ctx),)


def shifted(array, axes, sizes, by):
    devices = math.prod(sizes)
    pairs = [(i, i + by) for i in range(devices) if 0 <= i + by < devices]
    return lax.ppermute(array, axes, pairs)


def block_tables(response_blocks, prompt_members, first_block, count):
    starts = jnp.cumsum(response_blocks) - response_blocks
    responses = response_blocks.shape[0]
    group = prompt_members.shape[1]
    listed = prompt_members.reshape(-1)
    owner = jnp.arange(listed.shape[0], dtype=jnp.int32) // group
    numbers = jnp.arange(responses, dtype=jnp.int32)
    hits = listed[:, None] == numbers[None, :]
    prompt_of = jnp.sum(jnp.where(hits, owner[:, None], 0), axis=0)
    blocks = first_block + jnp.arange(count, dtype=jnp.int32)
    before = starts[None, :] <= blocks[:, None]
    first = jnp.max(jnp.where(before, starts[None, :], 0), axis=1)
    current = jnp.sum(before.astype(jnp.int32), axis=1) - 1
    chosen = numbers[None, :] == current[:, None]
    prompt_block = jnp.sum(jnp.where(chosen, prompt_of[None, :], 0), axis=1)
    return first, prompt_block


CH = 128


def tile_body(need_ref, q_ref, do_ref, k_ref, v_ref, n_ref, d_ref, lo_ref, hi_ref, dq_ref, dkv_ref):
    f32, bf16 = jnp.float32, jnp.bfloat16
    scale = 1.0 / math.sqrt(HD)
    nt = (((1,), (1,)), ((), ()))
    rows, span, grp = q_ref.shape[0], k_ref.shape[0], n_ref.shape[1]
    nrm, dlt = n_ref[0], d_ref[0]
    lo, hi = lo_ref[...], hi_ref[...]
    dq_ref[...] = jnp.zeros_like(dq_ref)

    def chunk(c, carry):
        ks = pl.ds(pl.multiple_of(c * CH, CH), CH)

        @pl.when(need_ref[c] > 0)
        def _():
            keys, values = k_ref[ks, :], v_ref[ks, :]
            u = c * CH + lax.broadcasted_iota(jnp.int32, (CH, rows), 0)
            allowed = (u >= lo) & (u <= hi)
            dk_acc = jnp.zeros((CH, HD), f32)
            dv_acc = jnp.zeros((CH, HD), f32)
            for r in range(grp):
                cols = slice(r * HD, (r + 1) * HD)
                qr, dor = q_ref[:, cols], do_ref[:, cols]
                st = lax.dot_general(keys, qr, nt, preferred_element_type=f32)
                wt = jnp.where(allowed, jnp.exp(st * scale - nrm[r : r + 1, :]), 0.0)
                dv_acc = dv_acc + jnp.dot(wt.astype(bf16), dor, preferred_element_type=f32)
                dwt = lax.dot_general(values, dor, nt, preferred_element_type=f32)
                dlt_r = wt * (dwt - dlt[r : r + 1, :])
                dk_acc = dk_acc + jnp.dot(dlt_r.astype(bf16), qr, preferred_element_type=f32)
                dq_ref[:, cols] += jnp.dot(
                    dlt_r.T.astype(bf16), keys, preferred_element_type=f32
                )
            dkv_ref[ks, 0:HD] = dk_acc
            dkv_ref[ks, HD : 2 * HD] = dv_acc

        @pl.when(need_ref[c] == 0)
        def _():
            dkv_ref[ks, :] = jnp.zeros((CH, 2 * HD), f32)

        return carry

    lax.fori_loop(0, span // CH, chunk, 0)

def tile_kernel(q, do, keys, values, norms, delta, lo, hi):
    tokens, lq = q.shape
    span, lk = keys.shape
    kvh, grp = norms.shape[0], norms.shape[1]
    width = grp * HD
    starts = jnp.arange(span // CH, dtype=jnp.int32) * CH
    need = jnp.any(
        (lo.reshape(-1)[None, :] <= starts[:, None] + CH - 1)
        & (hi.reshape(-1)[None, :] >= starts[:, None]),
        axis=1,
    ).astype(jnp.int32)
    flops = 10 * tokens * span * HD * kvh * grp
    grid_spec = pltpu.PrefetchScalarGridSpec(
        num_scalar_prefetch=1,
        grid=(kvh,),
        in_specs=[
            pl.BlockSpec((tokens, width), lambda g, n: (0, g)),
            pl.BlockSpec((tokens, width), lambda g, n: (0, g)),
            pl.BlockSpec((span, HD), lambda g, n: (0, g)),
            pl.BlockSpec((span, HD), lambda g, n: (0, g)),
            pl.BlockSpec((1, grp, tokens), lambda g, n: (g, 0, 0)),
            pl.BlockSpec((1, grp, tokens), lambda g, n: (g, 0, 0)),
            pl.BlockSpec((1, tokens), lambda g, n: (0, 0)),
            pl.BlockSpec((1, tokens), lambda g, n: (0, 0)),
        ],
        out_specs=[
            pl.BlockSpec((tokens, width), lambda g, n: (0, g)),
            pl.BlockSpec((span, 2 * HD), lambda g, n: (0, g)),
        ],
    )
    return pl.pallas_call(
        tile_body,
        grid_spec=grid_spec,
        out_shape=[
            jax.ShapeDtypeStruct((tokens, lq), jnp.float32),
            jax.ShapeDtypeStruct((span, 2 * lk), jnp.float32),
        ],
        compiler_params=pltpu.CompilerParams(dimension_semantics=("arbitrary",)),
        cost_estimate=pl.CostEstimate(
            flops=flops,
            transcendentals=tokens * span * kvh * grp,
            bytes_accessed=4 * tokens * lq * 2 + 2 * span * lk * 6,
        ),
    )(need, q, do, keys, values, norms, delta, lo, hi)


def make_shards(parts):
    names = tuple(n for n, _ in parts)
    sizes = tuple(s for _, s in parts)

    def shards(
        query_rows,
        key_rows,
        value_rows,
        attn_output,
        out_grad,
        log_norm,
        prefix_keys,
        prefix_values,
        response_blocks,
        prompt_members,
    ):
        f32, bf16 = jnp.float32, jnp.bfloat16
        nh = lax.axis_size("head")
        rows, qw = query_rows.shape
        kw = key_rows.shape[1]
        all_heads = qw // HD
        scale = 1.0 / math.sqrt(HD)

        delta_rows = jnp.einsum(
            "thd,thd->th",
            out_grad.reshape(rows, all_heads, HD),
            attn_output.reshape(rows, all_heads, HD),
            preferred_element_type=f32,
        )
        packed = jnp.concatenate(
            [
                query_rows.reshape(rows, nh, qw // nh),
                out_grad.reshape(rows, nh, qw // nh),
                key_rows.reshape(rows, nh, kw // nh),
                value_rows.reshape(rows, nh, kw // nh),
            ],
            axis=2,
        )
        got = lax.all_to_all(packed, "head", split_axis=1, concat_axis=0, tiled=True)
        deltas = lax.all_to_all(
            delta_rows.reshape(rows, nh, all_heads // nh),
            "head",
            split_axis=1,
            concat_axis=0,
            tiled=True,
        )
        tokens = got.shape[0]
        got = got.reshape(tokens, -1)
        lq, lk = qw // nh, kw // nh
        kvh = lk // HD
        grp = (lq // HD) // kvh
        q = got[:, :lq].reshape(tokens, kvh, grp, HD)
        do = got[:, lq : 2 * lq].reshape(tokens, kvh, grp, HD)
        k = got[:, 2 * lq : 2 * lq + lk].reshape(tokens, kvh, HD)
        v = got[:, 2 * lq + lk :].reshape(tokens, kvh, HD)
        norms = log_norm.reshape(kvh, grp, tokens)
        delta = deltas.reshape(tokens, kvh * grp).T.reshape(kvh, grp, tokens)

        position = lax.axis_index(names)
        base = position * tokens
        nblk = tokens // BLK
        first, prompt_block = block_tables(
            response_blocks, prompt_members, position * nblk, nblk
        )
        local_start = jnp.repeat(first * BLK, BLK) - base

        kv = got[:, 2 * lq :]
        kv_prior = shifted(kv, names, sizes, 1)
        t = jnp.arange(tokens, dtype=jnp.int32).reshape(1, tokens)
        ls = local_start.reshape(1, tokens).astype(jnp.int32)
        dq, dkv = tile_kernel(
            got[:, :lq], got[:, lq : 2 * lq], kv[:, :lk], kv[:, lk:], norms, delta, ls, t
        )
        dq_b, dkv_b = tile_kernel(
            got[:, :lq],
            got[:, lq : 2 * lq],
            kv_prior[:, :lk],
            kv_prior[:, lk:],
            norms,
            delta,
            ls + tokens,
            jnp.full((1, tokens), tokens - 1, jnp.int32),
        )
        back = shifted(dkv_b.astype(bf16), names, sizes, -1)
        dq = dq + dq_b

        pkv, _ = lax.optimization_barrier(
            (jnp.concatenate([prefix_keys, prefix_values], axis=1), got)
        )
        nctx = math.prod(sizes)
        pkv = lax.all_to_all(
            jnp.broadcast_to(pkv[None], (nctx,) + pkv.shape),
            names,
            split_axis=0,
            concat_axis=0,
            tiled=True,
        ).reshape(nctx * pkv.shape[0], pkv.shape[1])
        pkv, dq = lax.optimization_barrier((pkv, dq))
        prompt_lo = (jnp.repeat(prompt_block, BLK) * PL).astype(jnp.int32)
        dq_p, pgrad = tile_kernel(
            got[:, :lq],
            got[:, lq : 2 * lq],
            pkv[:, :lk],
            pkv[:, lk:],
            norms,
            delta,
            prompt_lo.reshape(1, tokens),
            (prompt_lo + PL - 1).reshape(1, tokens),
        )
        pgrad = lax.all_to_all(
            pgrad.reshape(nctx, -1, pgrad.shape[1]),
            names,
            split_axis=0,
            concat_axis=0,
            tiled=True,
        ).sum(axis=0)
        pgrad = pgrad.reshape(-1, kvh, 2, HD)

        kv_grad = (dkv + back.astype(f32)).reshape(tokens, kvh, 2, HD)
        return (
            ((dq + dq_p) * scale).astype(bf16),
            (kv_grad[:, :, 0] * scale).astype(bf16).reshape(tokens, lk),
            kv_grad[:, :, 1].astype(bf16).reshape(tokens, lk),
            (pgrad[:, :, 0] * scale).astype(bf16).reshape(-1, lk),
            pgrad[:, :, 1].astype(bf16).reshape(-1, lk),
        )

    return shards, names


def solution(mesh):
    parts = ctx_axes(mesh)
    devices = np.asarray(mesh.devices).reshape(
        tuple(s for _, s in parts) + (mesh.shape["head"],)
    )
    sub = Mesh(devices, tuple(n for n, _ in parts) + ("head",))
    shards, ctx = make_shards(parts)
    rows = P(ctx + ("head",), None)
    grid = P(ctx, "head")
    placed = (
        rows,
        rows,
        rows,
        rows,
        rows,
        P("head", ctx),
        grid,
        grid,
        P(),
        P(),
    )
    return jax.shard_map(
        shards,
        mesh=sub,
        in_specs=placed,
        out_specs=(grid,) * 5,
        check_vma=False,
    )
```

```python
import math

import jax
import jax.numpy as jnp
import numpy as np
from jax import lax
from jax.experimental import pallas as pl
from jax.experimental.pallas import tpu as pltpu
from jax.sharding import Mesh
from jax.sharding import PartitionSpec as P

HD = 128
BLK = 32
PL = 128

CTX_PARTS = (("z", 8), ("yh", 2), ("x", 4))


def ctx_axes(mesh):
    ctx = mesh.shape["ctx"]
    if ctx == math.prod(n for _, n in CTX_PARTS):
        return CTX_PARTS
    return (("c", ctx),)


def shifted(array, axes, sizes, by):
    devices = math.prod(sizes)
    pairs = [(i, i + by) for i in range(devices) if 0 <= i + by < devices]
    return lax.ppermute(array, axes, pairs)


def block_tables(response_blocks, prompt_members, first_block, count):
    starts = jnp.cumsum(response_blocks) - response_blocks
    responses = response_blocks.shape[0]
    group = prompt_members.shape[1]
    listed = prompt_members.reshape(-1)
    owner = jnp.arange(listed.shape[0], dtype=jnp.int32) // group
    numbers = jnp.arange(responses, dtype=jnp.int32)
    hits = listed[:, None] == numbers[None, :]
    prompt_of = jnp.sum(jnp.where(hits, owner[:, None], 0), axis=0)
    blocks = first_block + jnp.arange(count, dtype=jnp.int32)
    before = starts[None, :] <= blocks[:, None]
    first = jnp.max(jnp.where(before, starts[None, :], 0), axis=1)
    current = jnp.sum(before.astype(jnp.int32), axis=1) - 1
    chosen = numbers[None, :] == current[:, None]
    prompt_block = jnp.sum(jnp.where(chosen, prompt_of[None, :], 0), axis=1)
    return first, prompt_block


CH = 128


def tile_body(need_ref, q_ref, do_ref, k_ref, v_ref, n_ref, d_ref, lo_ref, hi_ref, dq_ref, dkv_ref):
    f32, bf16 = jnp.float32, jnp.bfloat16
    scale = 1.0 / math.sqrt(HD)
    nt = (((1,), (1,)), ((), ()))
    rows, span, grp = q_ref.shape[0], k_ref.shape[0], n_ref.shape[1]
    nrm, dlt = n_ref[0], d_ref[0]
    lo, hi = lo_ref[...], hi_ref[...]
    dq_ref[...] = jnp.zeros_like(dq_ref)

    def chunk(c, carry):
        ks = pl.ds(pl.multiple_of(c * CH, CH), CH)

        @pl.when(need_ref[c] > 0)
        def _():
            keys, values = k_ref[ks, :], v_ref[ks, :]
            u = c * CH + lax.broadcasted_iota(jnp.int32, (CH, rows), 0)
            allowed = (u >= lo) & (u <= hi)
            dk_acc = jnp.zeros((CH, HD), f32)
            dv_acc = jnp.zeros((CH, HD), f32)
            for r in range(grp):
                cols = slice(r * HD, (r + 1) * HD)
                qr, dor = q_ref[:, cols], do_ref[:, cols]
                st = lax.dot_general(keys, qr, nt, preferred_element_type=f32)
                wt = jnp.where(allowed, jnp.exp(st * scale - nrm[r : r + 1, :]), 0.0)
                dv_acc = dv_acc + jnp.dot(wt.astype(bf16), dor, preferred_element_type=f32)
                dwt = lax.dot_general(values, dor, nt, preferred_element_type=f32)
                dlt_r = wt * (dwt - dlt[r : r + 1, :])
                dk_acc = dk_acc + jnp.dot(dlt_r.astype(bf16), qr, preferred_element_type=f32)
                dq_ref[:, cols] += jnp.dot(
                    dlt_r.T.astype(bf16), keys, preferred_element_type=f32
                )
            dkv_ref[ks, 0:HD] = dk_acc
            dkv_ref[ks, HD : 2 * HD] = dv_acc

        @pl.when(need_ref[c] == 0)
        def _():
            dkv_ref[ks, :] = jnp.zeros((CH, 2 * HD), f32)

        return carry

    lax.fori_loop(0, span // CH, chunk, 0)

def tile_kernel(q, do, keys, values, norms, delta, lo, hi):
    tokens, lq = q.shape
    span, lk = keys.shape
    kvh, grp = norms.shape[0], norms.shape[1]
    width = grp * HD
    starts = jnp.arange(span // CH, dtype=jnp.int32) * CH
    need = jnp.any(
        (lo.reshape(-1)[None, :] <= starts[:, None] + CH - 1)
        & (hi.reshape(-1)[None, :] >= starts[:, None]),
        axis=1,
    ).astype(jnp.int32)
    flops = 10 * tokens * span * HD * kvh * grp
    grid_spec = pltpu.PrefetchScalarGridSpec(
        num_scalar_prefetch=1,
        grid=(kvh,),
        in_specs=[
            pl.BlockSpec((tokens, width), lambda g, n: (0, g)),
            pl.BlockSpec((tokens, width), lambda g, n: (0, g)),
            pl.BlockSpec((span, HD), lambda g, n: (0, g)),
            pl.BlockSpec((span, HD), lambda g, n: (0, g)),
            pl.BlockSpec((1, grp, tokens), lambda g, n: (g, 0, 0)),
            pl.BlockSpec((1, grp, tokens), lambda g, n: (g, 0, 0)),
            pl.BlockSpec((1, tokens), lambda g, n: (0, 0)),
            pl.BlockSpec((1, tokens), lambda g, n: (0, 0)),
        ],
        out_specs=[
            pl.BlockSpec((tokens, width), lambda g, n: (0, g)),
            pl.BlockSpec((span, 2 * HD), lambda g, n: (0, g)),
        ],
    )
    return pl.pallas_call(
        tile_body,
        grid_spec=grid_spec,
        out_shape=[
            jax.ShapeDtypeStruct((tokens, lq), jnp.float32),
            jax.ShapeDtypeStruct((span, 2 * lk), jnp.float32),
        ],
        compiler_params=pltpu.CompilerParams(dimension_semantics=("arbitrary",)),
        cost_estimate=pl.CostEstimate(
            flops=flops,
            transcendentals=tokens * span * kvh * grp,
            bytes_accessed=4 * tokens * lq * 2 + 2 * span * lk * 6,
        ),
    )(need, q, do, keys, values, norms, delta, lo, hi)


def make_shards(parts):
    names = tuple(n for n, _ in parts)
    sizes = tuple(s for _, s in parts)

    def shards(
        query_rows,
        key_rows,
        value_rows,
        attn_output,
        out_grad,
        log_norm,
        prefix_keys,
        prefix_values,
        response_blocks,
        prompt_members,
    ):
        f32, bf16 = jnp.float32, jnp.bfloat16
        nh = lax.axis_size("head")
        rows, qw = query_rows.shape
        kw = key_rows.shape[1]
        all_heads = qw // HD
        scale = 1.0 / math.sqrt(HD)

        delta_rows = jnp.einsum(
            "thd,thd->th",
            out_grad.reshape(rows, all_heads, HD),
            attn_output.reshape(rows, all_heads, HD),
            preferred_element_type=f32,
        )
        packed = jnp.concatenate(
            [
                query_rows.reshape(rows, nh, qw // nh),
                out_grad.reshape(rows, nh, qw // nh),
                key_rows.reshape(rows, nh, kw // nh),
                value_rows.reshape(rows, nh, kw // nh),
            ],
            axis=2,
        )
        got = lax.all_to_all(packed, "head", split_axis=1, concat_axis=0, tiled=True)
        deltas = lax.all_to_all(
            delta_rows.reshape(rows, nh, all_heads // nh),
            "head",
            split_axis=1,
            concat_axis=0,
            tiled=True,
        )
        tokens = got.shape[0]
        got = got.reshape(tokens, -1)
        lq, lk = qw // nh, kw // nh
        kvh = lk // HD
        grp = (lq // HD) // kvh
        q = got[:, :lq].reshape(tokens, kvh, grp, HD)
        do = got[:, lq : 2 * lq].reshape(tokens, kvh, grp, HD)
        k = got[:, 2 * lq : 2 * lq + lk].reshape(tokens, kvh, HD)
        v = got[:, 2 * lq + lk :].reshape(tokens, kvh, HD)
        norms = log_norm.reshape(kvh, grp, tokens)
        delta = deltas.reshape(tokens, kvh * grp).T.reshape(kvh, grp, tokens)

        position = lax.axis_index(names)
        base = position * tokens
        nblk = tokens // BLK
        first, prompt_block = block_tables(
            response_blocks, prompt_members, position * nblk, nblk
        )
        local_start = jnp.repeat(first * BLK, BLK) - base

        kv = got[:, 2 * lq :]
        kv_prior = shifted(kv, names, sizes, 1)
        t = jnp.arange(tokens, dtype=jnp.int32).reshape(1, tokens)
        ls = local_start.reshape(1, tokens).astype(jnp.int32)
        dq, dkv = tile_kernel(
            got[:, :lq], got[:, lq : 2 * lq], kv[:, :lk], kv[:, lk:], norms, delta, ls, t
        )
        dq_b, dkv_b = tile_kernel(
            got[:, :lq],
            got[:, lq : 2 * lq],
            kv_prior[:, :lk],
            kv_prior[:, lk:],
            norms,
            delta,
            ls + tokens,
            jnp.full((1, tokens), tokens - 1, jnp.int32),
        )
        back = shifted(dkv_b.astype(bf16), names, sizes, -1)
        dq = dq + dq_b

        pkv, _ = lax.optimization_barrier(
            (jnp.concatenate([prefix_keys, prefix_values], axis=1), got)
        )
        nctx = math.prod(sizes)
        pkv = lax.all_to_all(
            jnp.broadcast_to(pkv[None], (nctx,) + pkv.shape),
            names,
            split_axis=0,
            concat_axis=0,
            tiled=True,
        ).reshape(nctx * pkv.shape[0], pkv.shape[1])
        pkv, dq = lax.optimization_barrier((pkv, dq))
        prompt_lo = (jnp.repeat(prompt_block, BLK) * PL).astype(jnp.int32)
        dq_p, pgrad = tile_kernel(
            got[:, :lq],
            got[:, lq : 2 * lq],
            pkv[:, :lk],
            pkv[:, lk:],
            norms,
            delta,
            prompt_lo.reshape(1, tokens),
            (prompt_lo + PL - 1).reshape(1, tokens),
        )
        pgrad, back = lax.optimization_barrier((pgrad, back))
        pgrad = lax.all_to_all(
            pgrad.reshape(nctx, -1, pgrad.shape[1]),
            names,
            split_axis=0,
            concat_axis=0,
            tiled=True,
        ).sum(axis=0)
        pgrad = pgrad.reshape(-1, kvh, 2, HD)

        kv_grad = (dkv + back.astype(f32)).reshape(tokens, kvh, 2, HD)
        return (
            ((dq + dq_p) * scale).astype(bf16),
            (kv_grad[:, :, 0] * scale).astype(bf16).reshape(tokens, lk),
            kv_grad[:, :, 1].astype(bf16).reshape(tokens, lk),
            (pgrad[:, :, 0] * scale).astype(bf16).reshape(-1, lk),
            pgrad[:, :, 1].astype(bf16).reshape(-1, lk),
        )

    return shards, names


def solution(mesh):
    parts = ctx_axes(mesh)
    devices = np.asarray(mesh.devices).reshape(
        tuple(s for _, s in parts) + (mesh.shape["head"],)
    )
    sub = Mesh(devices, tuple(n for n, _ in parts) + ("head",))
    shards, ctx = make_shards(parts)
    rows = P(ctx + ("head",), None)
    grid = P(ctx, "head")
    placed = (
        rows,
        rows,
        rows,
        rows,
        rows,
        P("head", ctx),
        grid,
        grid,
        P(),
        P(),
    )
    return jax.shard_map(
        shards,
        mesh=sub,
        in_specs=placed,
        out_specs=(grid,) * 5,
        check_vma=False,
    )
```

```python
import math

import jax
import jax.numpy as jnp
import numpy as np
from jax import lax
from jax.experimental import pallas as pl
from jax.experimental.pallas import tpu as pltpu
from jax.sharding import Mesh
from jax.sharding import PartitionSpec as P

HD = 128
BLK = 32
PL = 128

CTX_PARTS = (("z", 8), ("yh", 2), ("x", 4))


def ctx_axes(mesh):
    ctx = mesh.shape["ctx"]
    if ctx == math.prod(n for _, n in CTX_PARTS):
        return CTX_PARTS
    return (("c", ctx),)


def shifted(array, axes, sizes, by):
    devices = math.prod(sizes)
    pairs = [(i, i + by) for i in range(devices) if 0 <= i + by < devices]
    return lax.ppermute(array, axes, pairs)


def block_tables(response_blocks, prompt_members, first_block, count):
    starts = jnp.cumsum(response_blocks) - response_blocks
    responses = response_blocks.shape[0]
    group = prompt_members.shape[1]
    listed = prompt_members.reshape(-1)
    owner = jnp.arange(listed.shape[0], dtype=jnp.int32) // group
    numbers = jnp.arange(responses, dtype=jnp.int32)
    hits = listed[:, None] == numbers[None, :]
    prompt_of = jnp.sum(jnp.where(hits, owner[:, None], 0), axis=0)
    blocks = first_block + jnp.arange(count, dtype=jnp.int32)
    before = starts[None, :] <= blocks[:, None]
    first = jnp.max(jnp.where(before, starts[None, :], 0), axis=1)
    current = jnp.sum(before.astype(jnp.int32), axis=1) - 1
    chosen = numbers[None, :] == current[:, None]
    prompt_block = jnp.sum(jnp.where(chosen, prompt_of[None, :], 0), axis=1)
    return first, prompt_block


CH = 128


def tile_body(need_ref, q_ref, do_ref, k_ref, v_ref, n_ref, d_ref, lo_ref, hi_ref, dq_ref, dkv_ref):
    f32, bf16 = jnp.float32, jnp.bfloat16
    scale = 1.0 / math.sqrt(HD)
    nt = (((1,), (1,)), ((), ()))
    rows, span, grp = q_ref.shape[0], k_ref.shape[0], n_ref.shape[1]
    nrm, dlt = n_ref[0], d_ref[0]
    lo, hi = lo_ref[...], hi_ref[...]
    dq_ref[...] = jnp.zeros_like(dq_ref)

    def chunk(c, carry):
        ks = pl.ds(pl.multiple_of(c * CH, CH), CH)

        @pl.when(need_ref[c] > 0)
        def _():
            keys, values = k_ref[ks, :], v_ref[ks, :]
            u = c * CH + lax.broadcasted_iota(jnp.int32, (CH, rows), 0)
            allowed = (u >= lo) & (u <= hi)
            dk_acc = jnp.zeros((CH, HD), f32)
            dv_acc = jnp.zeros((CH, HD), f32)
            for r in range(grp):
                cols = slice(r * HD, (r + 1) * HD)
                qr, dor = q_ref[:, cols], do_ref[:, cols]
                st = lax.dot_general(keys, qr, nt, preferred_element_type=f32)
                wt = jnp.where(allowed, jnp.exp(st * scale - nrm[r : r + 1, :]), 0.0)
                dv_acc = dv_acc + jnp.dot(wt.astype(bf16), dor, preferred_element_type=f32)
                dwt = lax.dot_general(values, dor, nt, preferred_element_type=f32)
                dlt_r = wt * (dwt - dlt[r : r + 1, :])
                dk_acc = dk_acc + jnp.dot(dlt_r.astype(bf16), qr, preferred_element_type=f32)
                dq_ref[:, cols] += jnp.dot(
                    dlt_r.T.astype(bf16), keys, preferred_element_type=f32
                )
            dkv_ref[ks, 0:HD] = dk_acc
            dkv_ref[ks, HD : 2 * HD] = dv_acc

        @pl.when(need_ref[c] == 0)
        def _():
            dkv_ref[ks, :] = jnp.zeros((CH, 2 * HD), f32)

        return carry

    lax.fori_loop(0, span // CH, chunk, 0)

def tile_kernel(q, do, keys, values, norms, delta, lo, hi):
    tokens, lq = q.shape
    span, lk = keys.shape
    kvh, grp = norms.shape[0], norms.shape[1]
    width = grp * HD
    starts = jnp.arange(span // CH, dtype=jnp.int32) * CH
    need = jnp.any(
        (lo.reshape(-1)[None, :] <= starts[:, None] + CH - 1)
        & (hi.reshape(-1)[None, :] >= starts[:, None]),
        axis=1,
    ).astype(jnp.int32)
    flops = 10 * tokens * span * HD * kvh * grp
    grid_spec = pltpu.PrefetchScalarGridSpec(
        num_scalar_prefetch=1,
        grid=(kvh,),
        in_specs=[
            pl.BlockSpec((tokens, width), lambda g, n: (0, g)),
            pl.BlockSpec((tokens, width), lambda g, n: (0, g)),
            pl.BlockSpec((span, HD), lambda g, n: (0, g)),
            pl.BlockSpec((span, HD), lambda g, n: (0, g)),
            pl.BlockSpec((1, grp, tokens), lambda g, n: (g, 0, 0)),
            pl.BlockSpec((1, grp, tokens), lambda g, n: (g, 0, 0)),
            pl.BlockSpec((1, tokens), lambda g, n: (0, 0)),
            pl.BlockSpec((1, tokens), lambda g, n: (0, 0)),
        ],
        out_specs=[
            pl.BlockSpec((tokens, width), lambda g, n: (0, g)),
            pl.BlockSpec((span, 2 * HD), lambda g, n: (0, g)),
        ],
    )
    return pl.pallas_call(
        tile_body,
        grid_spec=grid_spec,
        out_shape=[
            jax.ShapeDtypeStruct((tokens, lq), jnp.float32),
            jax.ShapeDtypeStruct((span, 2 * lk), jnp.float32),
        ],
        compiler_params=pltpu.CompilerParams(dimension_semantics=("arbitrary",)),
        cost_estimate=pl.CostEstimate(
            flops=flops,
            transcendentals=tokens * span * kvh * grp,
            bytes_accessed=4 * tokens * lq * 2 + 2 * span * lk * 6,
        ),
    )(need, q, do, keys, values, norms, delta, lo, hi)


def make_shards(parts):
    names = tuple(n for n, _ in parts)
    sizes = tuple(s for _, s in parts)

    def shards(
        query_rows,
        key_rows,
        value_rows,
        attn_output,
        out_grad,
        log_norm,
        prefix_keys,
        prefix_values,
        response_blocks,
        prompt_members,
    ):
        f32, bf16 = jnp.float32, jnp.bfloat16
        nh = lax.axis_size("head")
        rows, qw = query_rows.shape
        kw = key_rows.shape[1]
        all_heads = qw // HD
        scale = 1.0 / math.sqrt(HD)

        delta_rows = jnp.einsum(
            "thd,thd->th",
            out_grad.reshape(rows, all_heads, HD),
            attn_output.reshape(rows, all_heads, HD),
            preferred_element_type=f32,
        )
        packed = jnp.concatenate(
            [
                query_rows.reshape(rows, nh, qw // nh),
                out_grad.reshape(rows, nh, qw // nh),
                key_rows.reshape(rows, nh, kw // nh),
                value_rows.reshape(rows, nh, kw // nh),
            ],
            axis=2,
        )
        got = lax.all_to_all(packed, "head", split_axis=1, concat_axis=0, tiled=True)
        deltas = lax.all_to_all(
            delta_rows.reshape(rows, nh, all_heads // nh),
            "head",
            split_axis=1,
            concat_axis=0,
            tiled=True,
        )
        tokens = got.shape[0]
        got = got.reshape(tokens, -1)
        lq, lk = qw // nh, kw // nh
        kvh = lk // HD
        grp = (lq // HD) // kvh
        q = got[:, :lq].reshape(tokens, kvh, grp, HD)
        do = got[:, lq : 2 * lq].reshape(tokens, kvh, grp, HD)
        k = got[:, 2 * lq : 2 * lq + lk].reshape(tokens, kvh, HD)
        v = got[:, 2 * lq + lk :].reshape(tokens, kvh, HD)
        norms = log_norm.reshape(kvh, grp, tokens)
        delta = deltas.reshape(tokens, kvh * grp).T.reshape(kvh, grp, tokens)

        position = lax.axis_index(names)
        base = position * tokens
        nblk = tokens // BLK
        first, prompt_block = block_tables(
            response_blocks, prompt_members, position * nblk, nblk
        )
        local_start = jnp.repeat(first * BLK, BLK) - base

        kv = got[:, 2 * lq :]
        kv_prior = shifted(kv, names, sizes, 1)
        t = jnp.arange(tokens, dtype=jnp.int32).reshape(1, tokens)
        ls = local_start.reshape(1, tokens).astype(jnp.int32)
        dq, dkv = tile_kernel(
            got[:, :lq], got[:, lq : 2 * lq], kv[:, :lk], kv[:, lk:], norms, delta, ls, t
        )
        dq_b, dkv_b = tile_kernel(
            got[:, :lq],
            got[:, lq : 2 * lq],
            kv_prior[:, :lk],
            kv_prior[:, lk:],
            norms,
            delta,
            ls + tokens,
            jnp.full((1, tokens), tokens - 1, jnp.int32),
        )
        back = shifted(dkv_b.astype(bf16), names, sizes, -1)
        dq = dq + dq_b

        pkv, _ = lax.optimization_barrier(
            (jnp.concatenate([prefix_keys, prefix_values], axis=1), got)
        )
        nctx = math.prod(sizes)
        pkv = lax.all_to_all(
            jnp.broadcast_to(pkv[None], (nctx,) + pkv.shape),
            names,
            split_axis=0,
            concat_axis=0,
            tiled=True,
        ).reshape(nctx * pkv.shape[0], pkv.shape[1])
        pkv, dq = lax.optimization_barrier((pkv, dq))
        prompt_lo = (jnp.repeat(prompt_block, BLK) * PL).astype(jnp.int32)
        dq_p, pgrad = tile_kernel(
            got[:, :lq],
            got[:, lq : 2 * lq],
            pkv[:, :lk],
            pkv[:, lk:],
            norms,
            delta,
            prompt_lo.reshape(1, tokens),
            (prompt_lo + PL - 1).reshape(1, tokens),
        )
        pgrad, back = lax.optimization_barrier((pgrad, back))
        pgrad = lax.all_to_all(
            pgrad.astype(bf16).reshape(nctx, -1, pgrad.shape[1]),
            names,
            split_axis=0,
            concat_axis=0,
            tiled=True,
        ).astype(f32).sum(axis=0)
        pgrad = pgrad.reshape(-1, kvh, 2, HD)

        kv_grad = (dkv + back.astype(f32)).reshape(tokens, kvh, 2, HD)
        return (
            ((dq + dq_p) * scale).astype(bf16),
            (kv_grad[:, :, 0] * scale).astype(bf16).reshape(tokens, lk),
            kv_grad[:, :, 1].astype(bf16).reshape(tokens, lk),
            (pgrad[:, :, 0] * scale).astype(bf16).reshape(-1, lk),
            pgrad[:, :, 1].astype(bf16).reshape(-1, lk),
        )

    return shards, names


def solution(mesh):
    parts = ctx_axes(mesh)
    devices = np.asarray(mesh.devices).reshape(
        tuple(s for _, s in parts) + (mesh.shape["head"],)
    )
    sub = Mesh(devices, tuple(n for n, _ in parts) + ("head",))
    shards, ctx = make_shards(parts)
    rows = P(ctx + ("head",), None)
    grid = P(ctx, "head")
    placed = (
        rows,
        rows,
        rows,
        rows,
        rows,
        P("head", ctx),
        grid,
        grid,
        P(),
        P(),
    )
    return jax.shard_map(
        shards,
        mesh=sub,
        in_specs=placed,
        out_specs=(grid,) * 5,
        check_vma=False,
    )
```
